512 devices in a mesh: sec: 4 (over x), lat: 8 (over z), lon: 16 (over y, core).
Axes of the slice: x: 4, y: 8, z: 8, core: 2. Of those that a mesh axis runs over, the one named last changes fastest.
Arguments:
- state: float32 [4, 75, 32, 2048], P('sec', None, 'lat', 'lon'), may hold values from -6 to 6
- mixing: bfloat16 [4, 75, 32, 2048], P('sec', None, 'lat', 'lon'), may hold values from 0.05 to 50
- eastward: bfloat16 [4, 75, 32, 2048], P('sec', None, 'lat', 'lon'), may hold values from -0.44921875 to 0.44921875
- northward: bfloat16 [4, 75, 32, 2048], P('sec', None, 'lat', 'lon'), may hold values from -0.44921875 to 0.44921875
- sea_mask: int32 [32, 2048], P('lat', 'lon'), may hold values 0 or 1
- weights: bfloat16 [4, 8, 16, 16, 16, 512], P('sec', 'lat', 'lon'), may hold values from -1.5 to 1.5
- source_block: int32 [4, 8, 16, 128, 4], P('sec', 'lat', 'lon'), may hold values from 0 to 31
- dest_block: int32 [4, 8, 16, 128, 4], P('sec', 'lat', 'lon'), may hold values from 0 to 31
- record_counts: int32 [4, 8, 16, 128], P('sec', 'lat', 'lon'), may hold values from 0 to 4, as said below
Outputs:
- adjoint: float32 [4, 75, 32, 2048], P('sec', None, 'lat', 'lon')
The draws below stay inside these ranges and needn't reach their ends.
Inputs may be any that keep to these rules, and one draw needn't show every extreme that they name: `record_counts`: in every section some receiving device has 4 live slots from every sending device.
All inputs are finite; a program needn't handle non-finite values. No bound on the sum of `sea_mask` on one device may be relied on, other than what follows from the above.
Results may differ from the reference program's by a relative error of at most 0.0003.
Values sent between devices are 32-bit elements; how exact they have to be, the bound alone decides.
No kernel may reach another device: no remote copies, remote signals or barrier semaphores. Data moves between devices by JAX's collectives and lax.ppermute only.
A program may use at most 64 MiB of HBM per device.

```python
import math
import jax
import jax.numpy as jnp
from jax import lax

LEV = 75
CY = 4
CX = 128
BLK = 16
CAP = 4
NCPL = 4
NSUB = 2
NY = 32
NX = 2048
PEERS = 128
SLOTS = 512
NBLK = 32
N_SEC = 4
N_LAT = 8
N_LON = 16


def draw_record_counts(key, part):
    drawn_counts = jax.random.randint(key, (N_SEC, N_LAT, N_LON, PEERS), 0, CAP + 1)
    chosen = jax.random.randint(jax.random.fold_in(key, 7), (N_SEC, 1, 1, 1), 0, N_LAT * N_LON)
    receiver_index = (jnp.arange(N_LAT, dtype=jnp.int32)[:, None] * N_LON + jnp.arange(N_LON, dtype=jnp.int32)[None, :])[None, :, :, None]
    return jnp.where(receiver_index == chosen, CAP, drawn_counts).astype(jnp.int32)


def draw_mixing(key, part):
    column_key = jax.random.fold_in(key, 11)
    level_key = jax.random.fold_in(key, 13)
    lower_log = math.log(0.05)
    upper_log = math.log(50.0)
    column_base = jnp.exp(jax.random.uniform(column_key, (N_SEC, 1, NY, NX), jnp.float32, minval=lower_log, maxval=upper_log))
    level_factor = jnp.exp(jax.random.uniform(level_key, (N_SEC, LEV, NY, NX), jnp.float32, minval=-0.7, maxval=0.7))
    return jnp.clip(column_base * level_factor, 0.05, 50.0).astype(jnp.bfloat16)


def touch_ends(values, key, least, high):
    longest = values.shape.index(max(values.shape))
    spots = []
    for shift in (0, 1):
        where = [jax.random.randint(jax.random.fold_in(key, axis), (), 0, length) for axis, length in enumerate(values.shape)]
        where[longest] = (where[longest] + shift) % values.shape[longest]
        spots.append(tuple(where))
    return values.at[spots[0]].set(least).at[spots[1]].set(high)


def level_of(own_key, shape, shards, low, largest):
    factor_of, own = 1.0, jax.random.fold_in(own_key, 6)
    for position, parts in shards:
        steps = jnp.exp(jax.random.uniform(jax.random.fold_in(own, position), (parts,), jnp.float32, low / len(shards), largest / len(shards)))
        factor_of = factor_of * jnp.repeat(steps, shape[position] // parts).reshape([-1 if axis == position else 1 for axis in range(len(shape))])
    return factor_of


def centred(own_key, shape, deviation, most, shards=(), held_as=jnp.bfloat16):
    result = deviation * jax.random.normal(own_key, shape, jnp.float32)
    if shards:
        result = result * level_of(own_key, shape, shards, -0.22, 0.18)
    return jnp.clip(result, -most, most).astype(held_as)


def setup_inputs(seed: int = 0) -> dict:
    seeds = jax.random.split(jax.random.key(seed), 10)
    state = centred(seeds[0], (N_SEC, LEV, NY, NX), 1.0, 6.0, ((0, 4), (2, 8), (3, 16)), jnp.float32)
    mixing = draw_mixing(jax.random.fold_in(seeds[9], 71), 0)
    eastward = jnp.clip(jax.random.uniform(seeds[2], (N_SEC, LEV, NY, NX), jnp.float32, -0.44921875, 0.44921875) * level_of(seeds[2], (N_SEC, LEV, NY, NX), ((0, 4), (2, 8), (3, 16)), -0.4, 0.0), -0.44921875, 0.44921875).astype(jnp.bfloat16)
    northward = jnp.clip(jax.random.uniform(seeds[3], (N_SEC, LEV, NY, NX), jnp.float32, -0.44921875, 0.44921875) * level_of(seeds[3], (N_SEC, LEV, NY, NX), ((0, 4), (2, 8), (3, 16)), -0.4, 0.0), -0.44921875, 0.44921875).astype(jnp.bfloat16)
    sea_mask = touch_ends((jax.random.randint(seeds[4], (NY, NX), 0, 10) < 7).astype(jnp.int32), jax.random.fold_in(seeds[4], 1), 0, 1)
    weights = centred(seeds[5], (N_SEC, N_LAT, N_LON, BLK, BLK, SLOTS), BLK ** -0.5, 1.5, ((0, 4), (1, 8), (2, 16)))
    source_block = touch_ends(jax.random.randint(seeds[6], (N_SEC, N_LAT, N_LON, PEERS, CAP), 0, NBLK), jax.random.fold_in(seeds[6], 1), 0, NBLK - 1).astype(jnp.int32)
    dest_block = touch_ends(jax.random.randint(seeds[7], (N_SEC, N_LAT, N_LON, PEERS, CAP), 0, NBLK), jax.random.fold_in(seeds[7], 1), 0, NBLK - 1).astype(jnp.int32)
    record_counts = draw_record_counts(jax.random.fold_in(seeds[9], 71), 0)
    return dict(state=state, mixing=mixing, eastward=eastward, northward=northward, sea_mask=sea_mask, weights=weights, source_block=source_block, dest_block=dest_block, record_counts=record_counts)


def column_solve(right, coeff):
    zero_row = jnp.zeros_like(coeff[:1])
    lower_band = jnp.concatenate([zero_row, coeff[1:]], axis=0)
    upper_band = jnp.concatenate([coeff[1:], zero_row], axis=0)
    centre = 1.0 + lower_band + upper_band

    def sweep_down(carried, entries):
        prior_c, prior_z = carried
        centre_k, beneath, overhead, right_k = entries
        pivot_value = centre_k + beneath * prior_c
        factor = -overhead / pivot_value
        partial_value = (right_k + beneath * prior_z) / pivot_value
        return (factor, partial_value), (factor, partial_value)

    start_pair = (jnp.zeros_like(right[0]), jnp.zeros_like(right[0]))
    _, (factors, partials) = lax.scan(sweep_down, start_pair, (centre, lower_band, upper_band, right))

    def sweep_up(carried, entries):
        factor, partial_value = entries
        solved_k = partial_value - factor * carried
        return solved_k, solved_k

    _, solved = lax.scan(sweep_up, jnp.zeros_like(right[0]), (factors, partials), reverse=True)
    return solved


def advect(mixed_adj, east_speed, north_speed):
    east_flux = east_speed * mixed_adj
    north_flux = north_speed * mixed_adj
    east_diff = jnp.roll(east_flux, -1, axis=2) - jnp.roll(east_flux, 1, axis=2)
    padded = jnp.pad(north_flux, ((0, 0), (1, 1), (0, 0)))
    north_diff = padded[:, 2:] - padded[:, :-2]
    return mixed_adj + 0.5 * (east_diff + north_diff)


def substep(adjoint, mixing, eastward, northward, keep):
    def section_step(entries):
        field_part, mix_part, east_part, north_part, keep_part = entries
        mixed_adj = column_solve(field_part, mix_part.astype(jnp.float32))
        return advect(mixed_adj, east_part.astype(jnp.float32), north_part.astype(jnp.float32)) * keep_part
    return lax.map(section_step, (adjoint, mixing, eastward, northward, keep))


def couple(adjoint, weight_table, source_block, dest_block, record_counts):
    section_count = adjoint.shape[0]
    peer_count = N_LAT * N_LON
    surface = adjoint[:, LEV - 1].reshape(section_count, N_LAT, CY, N_LON, CX)
    surface = surface.transpose(0, 1, 3, 2, 4).reshape(section_count, N_LAT, N_LON, NBLK, BLK)
    sources = source_block.reshape(section_count, N_LAT, N_LON, SLOTS)
    gathered = jnp.take_along_axis(surface, sources[..., None], axis=3)
    contribution = jnp.einsum("saodiz,saozi->saodz", weight_table, gathered, precision=lax.Precision.HIGHEST)
    outgoing = contribution.reshape(section_count, peer_count, BLK, peer_count, CAP)
    arrived = outgoing.transpose(0, 3, 1, 4, 2)
    counts_view = record_counts.reshape(section_count, peer_count, peer_count)
    live_slot = jnp.arange(CAP, dtype=jnp.int32)[None, None, None, :] < counts_view[..., None]
    air_mask = (jnp.arange(section_count, dtype=jnp.int32) < section_count - 1)[:, None, None, None]
    arrived_live = arrived * jnp.logical_and(live_slot, air_mask)[..., None].astype(jnp.float32)
    receiver_ids = jnp.arange(section_count * peer_count, dtype=jnp.int32).reshape(section_count, peer_count, 1, 1)
    segment_ids = receiver_ids * NBLK + dest_block.reshape(section_count, peer_count, peer_count, CAP).astype(jnp.int32)
    accumulated = jax.ops.segment_sum(arrived_live.reshape(-1, BLK), segment_ids.reshape(-1),
                                      num_segments=section_count * peer_count * NBLK)
    accumulated = accumulated.reshape(section_count, peer_count, NBLK, BLK).sum(axis=0)
    forcing = accumulated.reshape(N_LAT, N_LON, CY, CX).transpose(0, 2, 1, 3).reshape(NY, NX)
    return forcing


def reference(state, mixing, eastward, northward, sea_mask, weights, source_block, dest_block, record_counts):
    section_count = state.shape[0]
    ocean_keep = sea_mask.astype(jnp.float32)
    keep = jnp.concatenate([jnp.ones((section_count - 1, NY, NX), jnp.float32), ocean_keep[None]], axis=0)
    weight_table = weights.astype(jnp.float32)
    adjoint = state
    for coupling in range(NCPL):
        for repeat in range(NSUB):
            adjoint = substep(adjoint, mixing, eastward, northward, keep)
        forcing = couple(adjoint, weight_table, source_block, dest_block, record_counts)
        adjoint = adjoint.at[section_count - 1, 0].add(forcing * ocean_keep)
    return adjoint
```

```python
import jax
import jax.numpy as jnp
from jax import lax
from jax.experimental import pallas as pl
from jax.experimental.pallas import tpu as pltpu
from jax.sharding import PartitionSpec as P

NCPL = 4
NSUB = 2
SKEW = 2


def extended(block, sides, width, periodic):
    for axis, dim in sides:
        count = lax.axis_size(axis)
        forward = [(i, i + 1) for i in range(count - 1)]
        if periodic:
            forward.append((count - 1, 0))
        backward = [(target, source) for source, target in forward]
        low = lax.ppermute(
            lax.slice_in_dim(block, block.shape[dim] - width, None, axis=dim), axis, forward
        )
        high = lax.ppermute(lax.slice_in_dim(block, 0, width, axis=dim), axis, backward)
        block = jnp.concatenate([low, block, high], axis=dim)
    return block


def _factor_kernel(a_ref, inv_ref, b_ref, c_ref):
    lev = a_ref.shape[0]
    prior_c = jnp.zeros(a_ref.shape[1:], jnp.float32)
    zero = jnp.zeros(a_ref.shape[1:], jnp.float32)
    for k in range(lev):
        lower = a_ref[k] if k >= 1 else zero
        upper = a_ref[k + 1] if k + 1 < lev else zero
        centre = 1.0 + lower + upper
        pivot = centre + lower * prior_c
        inv = 1.0 / pivot
        factor = -upper / pivot
        inv_ref[k] = inv
        b_ref[k] = lower * inv
        c_ref[k] = factor
        prior_c = factor


def _solve_kernel(x_ref, inv_ref, b_ref, c_ref, o_ref):
    lev = x_ref.shape[0]

    def down(k, z):
        z = x_ref[k] * inv_ref[k] + b_ref[k] * z
        o_ref[k] = z
        return z

    def up(i, x):
        k = lev - 1 - i
        x = o_ref[k] - c_ref[k] * x
        o_ref[k] = x
        return x

    zero = jnp.zeros(x_ref.shape[1:], jnp.float32)
    lax.fori_loop(0, lev, down, zero, unroll=5)
    lax.fori_loop(0, lev, up, zero, unroll=5)


def factorise(coeff):
    shape = jax.ShapeDtypeStruct(coeff.shape, jnp.float32)
    size = coeff.size
    return pl.pallas_call(
        _factor_kernel,
        out_shape=(shape, shape, shape),
        cost_estimate=pl.CostEstimate(flops=8 * size, bytes_accessed=16 * size, transcendentals=0),
    )(coeff)


def column_solve(right, inv, lower, factor):
    size = right.size
    return pl.pallas_call(
        _solve_kernel,
        out_shape=jax.ShapeDtypeStruct(right.shape, jnp.float32),
        cost_estimate=pl.CostEstimate(flops=6 * size, bytes_accessed=20 * size, transcendentals=0),
    )(right, inv, lower, factor)


def advect(mixed_adj, east_speed, north_speed):
    east_flux = east_speed * mixed_adj
    north_flux = north_speed * mixed_adj
    east_rim = extended(east_flux, (("lon", 2),), 1, True)
    north_rim = extended(north_flux, (("lat", 1),), 1, False)
    east_diff = east_rim[:, :, 2:] - east_rim[:, :, :-2]
    north_diff = north_rim[:, 2:, :] - north_rim[:, :-2, :]
    return mixed_adj + 0.5 * (east_diff + north_diff)


def couple(field_part, weight_table, source_block, peer_count):
    block_cells = weight_table.shape[0]
    capacity = source_block.shape[-1]
    surface = field_part[-1].reshape(-1, block_cells)
    gathered = jnp.take(surface, source_block.reshape(-1), axis=0)
    contribution = jnp.einsum("diz,zi->dz", weight_table, gathered, precision=lax.Precision.HIGHEST)
    return lax.all_to_all(
        contribution.reshape(block_cells, peer_count, capacity),
        ("lat", "lon"),
        split_axis=1,
        concat_axis=1,
        tiled=True,
    )


def reduce_forcing(received, one_hot):
    block_cells = received.shape[0]
    arrived = received.reshape(block_cells, -1)
    accumulated = jnp.dot(
        arrived, one_hot, precision=lax.Precision.HIGHEST, preferred_element_type=jnp.float32
    )
    section_count = lax.axis_size("sec")
    return [lax.ppermute(accumulated, "sec", [(s, section_count - 1)]) for s in range(section_count - 1)]


def forcing_field(parts, shape):
    total = parts[0]
    for part in parts[1:]:
        total = total + part
    return total.T.reshape(shape)


def local(
    state, mixing, eastward, northward, sea_mask, weights, source_block, dest_block, record_counts
):
    section = lax.axis_index("sec")
    section_count = lax.axis_size("sec")
    is_ocean = section == section_count - 1
    ocean_keep = sea_mask.astype(jnp.float32)
    keep_factor = jnp.where(is_ocean, ocean_keep, jnp.ones_like(ocean_keep))
    field_part = state[0]
    inv, lower, factor = factorise(mixing[0].astype(jnp.float32))
    east_part = eastward[0].astype(jnp.float32)
    north_part = northward[0].astype(jnp.float32)

    weight_table = weights[0, 0, 0].astype(jnp.float32)
    block_count = field_part.shape[1] * field_part.shape[2] // weight_table.shape[0]
    capacity = source_block.shape[-1]
    live_slot = (
        jnp.arange(capacity, dtype=jnp.int32)[None, :] < record_counts[0, 0, 0][:, None]
    ).reshape(-1)
    matches = dest_block.reshape(-1)[:, None] == jnp.arange(block_count, dtype=jnp.int32)[None, :]
    one_hot = jnp.logical_and(matches, live_slot[:, None]).astype(jnp.float32)

    def substep(x):
        mixed_adj = column_solve(x, inv, lower, factor)
        return advect(mixed_adj, east_part, north_part) * keep_factor

    total_steps = NCPL * NSUB
    peer_count = record_counts.shape[-1]
    plane = field_part.shape[1:]
    in_flight = {}
    saved = None
    for step in range(total_steps + SKEW):
        advanced = substep(field_part)
        if step < SKEW:
            field_part = jnp.where(is_ocean, field_part, advanced)
        else:
            field_part = advanced
        for c, (stage, value) in list(in_flight.items()):
            if stage == 0:
                value, _ = lax.optimization_barrier((value, field_part))
                in_flight[c] = (1, reduce_forcing(value, one_hot))
        air_done = step + 1
        if air_done <= total_steps and air_done % NSUB == 0:
            in_flight[air_done // NSUB - 1] = (
                0, couple(field_part, weight_table, source_block, peer_count))
        if step == total_steps - 1:
            saved = field_part
        ocean_done = step - SKEW + 1
        if ocean_done >= 1 and ocean_done % NSUB == 0:
            stage, parts = in_flight.pop(ocean_done // NSUB - 1)
            forcing = forcing_field(parts, plane)
            field_part = field_part.at[0].add(
                jnp.where(is_ocean, forcing * ocean_keep, jnp.zeros_like(forcing))
            )
    field_part = jnp.where(is_ocean, field_part, saved)
    return field_part[None]


def solution(mesh):
    in_specs = (
        P("sec", None, "lat", "lon"),
        P("sec", None, "lat", "lon"),
        P("sec", None, "lat", "lon"),
        P("sec", None, "lat", "lon"),
        P("lat", "lon"),
        P("sec", "lat", "lon", None, None, None),
        P("sec", "lat", "lon", None, None),
        P("sec", "lat", "lon", None, None),
        P("sec", "lat", "lon", None),
    )
    out_specs = P("sec", None, "lat", "lon")
    return jax.shard_map(local, mesh=mesh, in_specs=in_specs, out_specs=out_specs, check_vma=False)
```

```python
import jax
import jax.numpy as jnp
from jax import lax
from jax.experimental import pallas as pl
from jax.experimental.pallas import tpu as pltpu
from jax.sharding import PartitionSpec as P

NCPL = 4
NSUB = 2
SKEW = 2


def extended(block, sides, width, periodic):
    for axis, dim in sides:
        count = lax.axis_size(axis)
        forward = [(i, i + 1) for i in range(count - 1)]
        if periodic:
            forward.append((count - 1, 0))
        backward = [(target, source) for source, target in forward]
        low = lax.ppermute(
            lax.slice_in_dim(block, block.shape[dim] - width, None, axis=dim), axis, forward
        )
        high = lax.ppermute(lax.slice_in_dim(block, 0, width, axis=dim), axis, backward)
        block = jnp.concatenate([low, block, high], axis=dim)
    return block


def _factor_kernel(a_ref, inv_ref, b_ref, c_ref):
    lev = a_ref.shape[0]
    prior_c = jnp.zeros(a_ref.shape[1:], jnp.float32)
    zero = jnp.zeros(a_ref.shape[1:], jnp.float32)
    for k in range(lev):
        lower = a_ref[k] if k >= 1 else zero
        upper = a_ref[k + 1] if k + 1 < lev else zero
        centre = 1.0 + lower + upper
        pivot = centre + lower * prior_c
        inv = 1.0 / pivot
        factor = -upper / pivot
        inv_ref[k] = inv
        b_ref[k] = lower * inv
        c_ref[k] = factor
        prior_c = factor


def _solve_kernel(x_ref, inv_ref, b_ref, c_ref, o_ref):
    lev = x_ref.shape[0]

    def down(k, z):
        z = x_ref[k] * inv_ref[k] + b_ref[k] * z
        o_ref[k] = z
        return z

    def up(i, x):
        k = lev - 1 - i
        x = o_ref[k] - c_ref[k] * x
        o_ref[k] = x
        return x

    zero = jnp.zeros(x_ref.shape[1:], jnp.float32)
    lax.fori_loop(0, lev, down, zero, unroll=5)
    lax.fori_loop(0, lev, up, zero, unroll=5)


def factorise(coeff):
    shape = jax.ShapeDtypeStruct(coeff.shape, jnp.float32)
    size = coeff.size
    return pl.pallas_call(
        _factor_kernel,
        out_shape=(shape, shape, shape),
        cost_estimate=pl.CostEstimate(flops=8 * size, bytes_accessed=16 * size, transcendentals=0),
    )(coeff)


def column_solve(right, inv, lower, factor):
    size = right.size
    return pl.pallas_call(
        _solve_kernel,
        out_shape=jax.ShapeDtypeStruct(right.shape, jnp.float32),
        cost_estimate=pl.CostEstimate(flops=6 * size, bytes_accessed=20 * size, transcendentals=0),
    )(right, inv, lower, factor)


def advect(mixed_adj, east_speed, north_speed):
    east_flux = east_speed * mixed_adj
    north_flux = north_speed * mixed_adj
    east_rim = extended(east_flux, (("lon", 2),), 1, True)
    north_rim = extended(north_flux, (("lat", 1),), 1, False)
    east_diff = east_rim[:, :, 2:] - east_rim[:, :, :-2]
    north_diff = north_rim[:, 2:, :] - north_rim[:, :-2, :]
    return mixed_adj + 0.5 * (east_diff + north_diff)


def redistribute(weights, source_block, block_count):
    block_cells = weights.shape[3]
    peer_count, capacity = source_block.shape[-2:]
    table = weights[0, 0, 0].astype(jnp.float32).reshape(block_cells * block_cells, peer_count, capacity)
    sources = source_block[0, 0, 0].astype(jnp.float32)[None]
    packed = lax.all_to_all(
        jnp.concatenate([table, sources], axis=0), ("lat", "lon"), split_axis=1, concat_axis=1, tiled=True
    )
    weight_in = packed[:-1].reshape(block_cells, block_cells, peer_count * capacity)
    sender = jnp.arange(peer_count, dtype=jnp.int32)[:, None] * block_count
    rows = (packed[-1].astype(jnp.int32) + sender).reshape(-1)
    return weight_in, rows


def couple(field_part, block_cells):
    surface = field_part[-1].reshape(-1, block_cells)
    return lax.all_gather(surface, ("lat", "lon"))


def reduce_forcing(gathered_surfaces, weight_in, rows, one_hot):
    block_cells = weight_in.shape[0]
    table = gathered_surfaces.reshape(-1, block_cells)
    picked = jnp.take(table, rows, axis=0)
    arrived = jnp.einsum("diz,zi->dz", weight_in, picked, precision=lax.Precision.HIGHEST)
    accumulated = jnp.dot(
        arrived, one_hot, precision=lax.Precision.HIGHEST, preferred_element_type=jnp.float32
    )
    section_count = lax.axis_size("sec")
    return [lax.ppermute(accumulated, "sec", [(s, section_count - 1)]) for s in range(section_count - 1)]


def forcing_field(parts, shape):
    total = parts[0]
    for part in parts[1:]:
        total = total + part
    return total.T.reshape(shape)


def local(
    state, mixing, eastward, northward, sea_mask, weights, source_block, dest_block, record_counts
):
    section = lax.axis_index("sec")
    section_count = lax.axis_size("sec")
    is_ocean = section == section_count - 1
    ocean_keep = sea_mask.astype(jnp.float32)
    keep_factor = jnp.where(is_ocean, ocean_keep, jnp.ones_like(ocean_keep))
    field_part = state[0]
    inv, lower, factor = factorise(mixing[0].astype(jnp.float32))
    east_part = eastward[0].astype(jnp.float32)
    north_part = northward[0].astype(jnp.float32)

    block_cells = weights.shape[3]
    block_count = field_part.shape[1] * field_part.shape[2] // block_cells
    weight_in, rows = redistribute(weights, source_block, block_count)
    capacity = source_block.shape[-1]
    live_slot = (
        jnp.arange(capacity, dtype=jnp.int32)[None, :] < record_counts[0, 0, 0][:, None]
    ).reshape(-1)
    matches = dest_block.reshape(-1)[:, None] == jnp.arange(block_count, dtype=jnp.int32)[None, :]
    one_hot = jnp.logical_and(matches, live_slot[:, None]).astype(jnp.float32)

    def substep(x):
        mixed_adj = column_solve(x, inv, lower, factor)
        return advect(mixed_adj, east_part, north_part) * keep_factor

    total_steps = NCPL * NSUB
    plane = field_part.shape[1:]
    in_flight = {}
    saved = None
    for step in range(total_steps + SKEW):
        advanced = substep(field_part)
        if step < SKEW:
            field_part = jnp.where(is_ocean, field_part, advanced)
        else:
            field_part = advanced
        for c, (stage, value) in list(in_flight.items()):
            if stage == 0:
                value, _ = lax.optimization_barrier((value, field_part))
                in_flight[c] = (1, reduce_forcing(value, weight_in, rows, one_hot))
        air_done = step + 1
        if air_done <= total_steps and air_done % NSUB == 0:
            in_flight[air_done // NSUB - 1] = (
                0, couple(field_part, block_cells))
        if step == total_steps - 1:
            saved = field_part
        ocean_done = step - SKEW + 1
        if ocean_done >= 1 and ocean_done % NSUB == 0:
            stage, parts = in_flight.pop(ocean_done // NSUB - 1)
            forcing = forcing_field(parts, plane)
            field_part = field_part.at[0].add(
                jnp.where(is_ocean, forcing * ocean_keep, jnp.zeros_like(forcing))
            )
    field_part = jnp.where(is_ocean, field_part, saved)
    return field_part[None]


def solution(mesh):
    in_specs = (
        P("sec", None, "lat", "lon"),
        P("sec", None, "lat", "lon"),
        P("sec", None, "lat", "lon"),
        P("sec", None, "lat", "lon"),
        P("lat", "lon"),
        P("sec", "lat", "lon", None, None, None),
        P("sec", "lat", "lon", None, None),
        P("sec", "lat", "lon", None, None),
        P("sec", "lat", "lon", None),
    )
    out_specs = P("sec", None, "lat", "lon")
    return jax.shard_map(local, mesh=mesh, in_specs=in_specs, out_specs=out_specs, check_vma=False)
```

```python
import jax
import jax.numpy as jnp
from jax import lax
from jax.experimental import pallas as pl
from jax.experimental.pallas import tpu as pltpu
from jax.sharding import PartitionSpec as P

NCPL = 4
NSUB = 2
SKEW = 2


def extended(block, sides, width, periodic):
    for axis, dim in sides:
        count = lax.axis_size(axis)
        forward = [(i, i + 1) for i in range(count - 1)]
        if periodic:
            forward.append((count - 1, 0))
        backward = [(target, source) for source, target in forward]
        low = lax.ppermute(
            lax.slice_in_dim(block, block.shape[dim] - width, None, axis=dim), axis, forward
        )
        high = lax.ppermute(lax.slice_in_dim(block, 0, width, axis=dim), axis, backward)
        block = jnp.concatenate([low, block, high], axis=dim)
    return block


def _factor_kernel(a_ref, inv_ref, b_ref, c_ref):
    lev = a_ref.shape[0]
    prior_c = jnp.zeros(a_ref.shape[1:], jnp.float32)
    zero = jnp.zeros(a_ref.shape[1:], jnp.float32)
    for k in range(lev):
        lower = a_ref[k] if k >= 1 else zero
        upper = a_ref[k + 1] if k + 1 < lev else zero
        centre = 1.0 + lower + upper
        pivot = centre + lower * prior_c
        inv = 1.0 / pivot
        factor = -upper / pivot
        inv_ref[k] = inv
        b_ref[k] = lower * inv
        c_ref[k] = factor
        prior_c = factor


def _solve_kernel(x_ref, inv_ref, b_ref, c_ref, o_ref):
    lev = x_ref.shape[0]

    def down(k, z):
        z = x_ref[k] * inv_ref[k] + b_ref[k] * z
        o_ref[k] = z
        return z

    def up(i, x):
        k = lev - 1 - i
        x = o_ref[k] - c_ref[k] * x
        o_ref[k] = x
        return x

    zero = jnp.zeros(x_ref.shape[1:], jnp.float32)
    lax.fori_loop(0, lev, down, zero, unroll=5)
    lax.fori_loop(0, lev, up, zero, unroll=5)


def factorise(coeff):
    shape = jax.ShapeDtypeStruct(coeff.shape, jnp.float32)
    size = coeff.size
    return pl.pallas_call(
        _factor_kernel,
        out_shape=(shape, shape, shape),
        cost_estimate=pl.CostEstimate(flops=8 * size, bytes_accessed=16 * size, transcendentals=0),
    )(coeff)


def column_solve(right, inv, lower, factor):
    size = right.size
    return pl.pallas_call(
        _solve_kernel,
        out_shape=jax.ShapeDtypeStruct(right.shape, jnp.float32),
        cost_estimate=pl.CostEstimate(flops=6 * size, bytes_accessed=20 * size, transcendentals=0),
    )(right, inv, lower, factor)


def advect(mixed_adj, east_speed, north_speed):
    east_flux = east_speed * mixed_adj
    north_flux = north_speed * mixed_adj
    east_rim = extended(east_flux, (("lon", 2),), 1, True)
    north_rim = extended(north_flux, (("lat", 1),), 1, False)
    east_diff = east_rim[:, :, 2:] - east_rim[:, :, :-2]
    north_diff = north_rim[:, 2:, :] - north_rim[:, :-2, :]
    return mixed_adj + 0.5 * (east_diff + north_diff)


def couple(field_part, weight_table, source_block, peer_count):
    block_cells = weight_table.shape[0]
    capacity = source_block.shape[-1]
    surface = field_part[-1].reshape(-1, block_cells)
    gathered = jnp.take(surface, source_block.reshape(-1), axis=0)
    contribution = jnp.einsum("diz,zi->dz", weight_table, gathered, precision=lax.Precision.HIGHEST)
    return lax.all_to_all(
        contribution.reshape(block_cells, peer_count, capacity),
        ("lat", "lon"),
        split_axis=1,
        concat_axis=1,
        tiled=True,
    )


def reduce_forcing(received, one_hot):
    block_cells = received.shape[0]
    arrived = received.reshape(block_cells, -1)
    accumulated = jnp.dot(
        arrived, one_hot, precision=lax.Precision.HIGHEST, preferred_element_type=jnp.float32
    )
    section_count = lax.axis_size("sec")
    return [lax.ppermute(accumulated, "sec", [(s, section_count - 1)]) for s in range(section_count - 1)]


def forcing_field(parts, shape):
    total = parts[0]
    for part in parts[1:]:
        total = total + part
    return total.T.reshape(shape)


def local(
    state, mixing, eastward, northward, sea_mask, weights, source_block, dest_block, record_counts
):
    section = lax.axis_index("sec")
    section_count = lax.axis_size("sec")
    is_ocean = section == section_count - 1
    ocean_keep = sea_mask.astype(jnp.float32)
    keep_factor = jnp.where(is_ocean, ocean_keep, jnp.ones_like(ocean_keep))
    field_part = state[0]

    weight_table = weights[0, 0, 0].astype(jnp.float32)
    peer_count = record_counts.shape[-1]
    block_count = field_part.shape[1] * field_part.shape[2] // weight_table.shape[0]
    capacity = source_block.shape[-1]
    live_slot = (
        jnp.arange(capacity, dtype=jnp.int32)[None, :] < record_counts[0, 0, 0][:, None]
    ).reshape(-1)
    matches = dest_block.reshape(-1)[:, None] == jnp.arange(block_count, dtype=jnp.int32)[None, :]
    one_hot = jnp.logical_and(matches, live_slot[:, None]).astype(jnp.float32)

    def widen(block, width):
        block = extended(block, (("lon", block.ndim - 1),), width, True)
        return extended(block, (("lat", block.ndim - 2),), width, False)

    def advect_inner(mixed_adj, east_speed, north_speed):
        east_flux = east_speed * mixed_adj
        north_flux = north_speed * mixed_adj
        east_diff = east_flux[:, 1:-1, 2:] - east_flux[:, 1:-1, :-2]
        north_diff = north_flux[:, 2:, 1:-1] - north_flux[:, :-2, 1:-1]
        return mixed_adj[:, 1:-1, 1:-1] + 0.5 * (east_diff + north_diff)

    halo = 2
    wide_mix = widen(mixing[0].astype(jnp.float32), halo)
    wide_east = widen(eastward[0].astype(jnp.float32), halo)
    wide_north = widen(northward[0].astype(jnp.float32), halo)
    wide_keep = widen(keep_factor[None], halo)
    inv_w, lower_w, factor_w = factorise(wide_mix)
    inner = (slice(None), slice(1, -1), slice(1, -1))
    inv_i, lower_i, factor_i = inv_w[inner], lower_w[inner], factor_w[inner]
    east_i, north_i, keep_i = wide_east[inner], wide_north[inner], wide_keep[inner]

    def first_substep(wide_x):
        mixed_adj = column_solve(wide_x, inv_w, lower_w, factor_w)
        return advect_inner(mixed_adj, wide_east, wide_north) * keep_i

    def second_substep(inner_x):
        mixed_adj = column_solve(inner_x, inv_i, lower_i, factor_i)
        return advect_inner(mixed_adj, east_i, north_i) * keep_factor

    total_steps = NCPL * NSUB
    plane = field_part.shape[1:]
    in_flight = {}
    saved = None
    for block in range((total_steps + SKEW) // NSUB):
        midway = first_substep(widen(field_part, halo))
        for c, (stage, value) in list(in_flight.items()):
            if stage == 0:
                value, _ = lax.optimization_barrier((value, midway))
                in_flight[c] = (1, reduce_forcing(value, one_hot))
        advanced = second_substep(midway)
        step = block * NSUB + NSUB - 1
        if step < SKEW:
            field_part = jnp.where(is_ocean, field_part, advanced)
        else:
            field_part = advanced
        air_done = step + 1
        if air_done <= total_steps and air_done % NSUB == 0:
            in_flight[air_done // NSUB - 1] = (
                0, couple(field_part, weight_table, source_block, peer_count))
        if step == total_steps - 1:
            saved = field_part
        ocean_done = step - SKEW + 1
        if ocean_done >= 1 and ocean_done % NSUB == 0:
            stage, parts = in_flight.pop(ocean_done // NSUB - 1)
            forcing = forcing_field(parts, plane)
            field_part = field_part.at[0].add(
                jnp.where(is_ocean, forcing * ocean_keep, jnp.zeros_like(forcing))
            )
    field_part = jnp.where(is_ocean, field_part, saved)
    return field_part[None]


def solution(mesh):
    in_specs = (
        P("sec", None, "lat", "lon"),
        P("sec", None, "lat", "lon"),
        P("sec", None, "lat", "lon"),
        P("sec", None, "lat", "lon"),
        P("lat", "lon"),
        P("sec", "lat", "lon", None, None, None),
        P("sec", "lat", "lon", None, None),
        P("sec", "lat", "lon", None, None),
        P("sec", "lat", "lon", None),
    )
    out_specs = P("sec", None, "lat", "lon")
    return jax.shard_map(local, mesh=mesh, in_specs=in_specs, out_specs=out_specs, check_vma=False)
```

```python
import jax
import jax.numpy as jnp
from jax import lax
from jax.experimental import pallas as pl
from jax.experimental.pallas import tpu as pltpu
from jax.sharding import PartitionSpec as P

NCPL = 4
NSUB = 2
SKEW = 2


def extended(block, sides, width, periodic):
    for axis, dim in sides:
        count = lax.axis_size(axis)
        forward = [(i, i + 1) for i in range(count - 1)]
        if periodic:
            forward.append((count - 1, 0))
        backward = [(target, source) for source, target in forward]
        low = lax.ppermute(
            lax.slice_in_dim(block, block.shape[dim] - width, None, axis=dim), axis, forward
        )
        high = lax.ppermute(lax.slice_in_dim(block, 0, width, axis=dim), axis, backward)
        block = jnp.concatenate([low, block, high], axis=dim)
    return block


def _factor_kernel(a_ref, inv_ref, b_ref, c_ref):
    lev = a_ref.shape[0]
    prior_c = jnp.zeros(a_ref.shape[1:], jnp.float32)
    zero = jnp.zeros(a_ref.shape[1:], jnp.float32)
    for k in range(lev):
        lower = a_ref[k] if k >= 1 else zero
        upper = a_ref[k + 1] if k + 1 < lev else zero
        centre = 1.0 + lower + upper
        pivot = centre + lower * prior_c
        inv = 1.0 / pivot
        factor = -upper / pivot
        inv_ref[k] = inv
        b_ref[k] = lower * inv
        c_ref[k] = factor
        prior_c = factor


def _solve_kernel(x_ref, inv_ref, b_ref, c_ref, o_ref):
    lev = x_ref.shape[0]

    def down(k, z):
        z = x_ref[k] * inv_ref[k] + b_ref[k] * z
        o_ref[k] = z
        return z

    def up(i, x):
        k = lev - 1 - i
        x = o_ref[k] - c_ref[k] * x
        o_ref[k] = x
        return x

    zero = jnp.zeros(x_ref.shape[1:], jnp.float32)
    lax.fori_loop(0, lev, down, zero, unroll=5)
    lax.fori_loop(0, lev, up, zero, unroll=5)


def factorise(coeff):
    shape = jax.ShapeDtypeStruct(coeff.shape, jnp.float32)
    size = coeff.size
    return pl.pallas_call(
        _factor_kernel,
        out_shape=(shape, shape, shape),
        cost_estimate=pl.CostEstimate(flops=8 * size, bytes_accessed=16 * size, transcendentals=0),
    )(coeff)


def column_solve(right, inv, lower, factor):
    size = right.size
    return pl.pallas_call(
        _solve_kernel,
        out_shape=jax.ShapeDtypeStruct(right.shape, jnp.float32),
        cost_estimate=pl.CostEstimate(flops=6 * size, bytes_accessed=20 * size, transcendentals=0),
    )(right, inv, lower, factor)


def advect(mixed_adj, east_speed, north_speed):
    east_flux = east_speed * mixed_adj
    north_flux = north_speed * mixed_adj
    east_rim = extended(east_flux, (("lon", 2),), 1, True)
    north_rim = extended(north_flux, (("lat", 1),), 1, False)
    east_diff = east_rim[:, :, 2:] - east_rim[:, :, :-2]
    north_diff = north_rim[:, 2:, :] - north_rim[:, :-2, :]
    return mixed_adj + 0.5 * (east_diff + north_diff)


def couple(field_part, weight_table, source_block, peer_count):
    block_cells = weight_table.shape[0]
    capacity = source_block.shape[-1]
    surface = field_part[-1].reshape(-1, block_cells)
    gathered = jnp.take(surface, source_block.reshape(-1), axis=0)
    contribution = jnp.einsum("diz,zi->dz", weight_table, gathered, precision=lax.Precision.HIGHEST)
    return lax.all_to_all(
        contribution.reshape(block_cells, peer_count, capacity),
        ("lat", "lon"),
        split_axis=1,
        concat_axis=1,
        tiled=True,
    )


def reduce_forcing(received, one_hot):
    block_cells = received.shape[0]
    arrived = received.reshape(block_cells, -1)
    accumulated = jnp.dot(
        arrived, one_hot, precision=lax.Precision.HIGHEST, preferred_element_type=jnp.float32
    )
    section_count = lax.axis_size("sec")
    return [lax.ppermute(accumulated, "sec", [(s, section_count - 1)]) for s in range(section_count - 1)]


def forcing_field(parts, shape):
    total = parts[0]
    for part in parts[1:]:
        total = total + part
    return total.T.reshape(shape)


def local(
    state, mixing, eastward, northward, sea_mask, weights, source_block, dest_block, record_counts
):
    section = lax.axis_index("sec")
    section_count = lax.axis_size("sec")
    is_ocean = section == section_count - 1
    ocean_keep = sea_mask.astype(jnp.float32)
    keep_factor = jnp.where(is_ocean, ocean_keep, jnp.ones_like(ocean_keep))
    field_part = state[0]

    weight_table = weights[0, 0, 0].astype(jnp.float32)
    peer_count = record_counts.shape[-1]
    block_count = field_part.shape[1] * field_part.shape[2] // weight_table.shape[0]
    capacity = source_block.shape[-1]
    live_slot = (
        jnp.arange(capacity, dtype=jnp.int32)[None, :] < record_counts[0, 0, 0][:, None]
    ).reshape(-1)
    matches = dest_block.reshape(-1)[:, None] == jnp.arange(block_count, dtype=jnp.int32)[None, :]
    one_hot = jnp.logical_and(matches, live_slot[:, None]).astype(jnp.float32)

    def widen(block, width):
        block = extended(block, (("lon", block.ndim - 1),), width, True)
        return extended(block, (("lat", block.ndim - 2),), width, False)

    def advect_inner(mixed_adj, east_speed, north_speed):
        east_flux = east_speed * mixed_adj
        north_flux = north_speed * mixed_adj
        east_diff = east_flux[:, 1:-1, 2:] - east_flux[:, 1:-1, :-2]
        north_diff = north_flux[:, 2:, 1:-1] - north_flux[:, :-2, 1:-1]
        return mixed_adj[:, 1:-1, 1:-1] + 0.5 * (east_diff + north_diff)

    halo = 2
    lev = mixing.shape[1]
    constants = jnp.concatenate(
        [
            mixing[0].astype(jnp.float32),
            eastward[0].astype(jnp.float32),
            northward[0].astype(jnp.float32),
            keep_factor[None],
        ],
        axis=0,
    )
    wide = widen(constants, halo)
    wide_mix, wide_east = wide[:lev], wide[lev : 2 * lev]
    wide_north, wide_keep = wide[2 * lev : 3 * lev], wide[3 * lev :]
    inv_w, lower_w, factor_w = factorise(wide_mix)
    inner = (slice(None), slice(1, -1), slice(1, -1))
    inv_i, lower_i, factor_i = inv_w[inner], lower_w[inner], factor_w[inner]
    east_i, north_i, keep_i = wide_east[inner], wide_north[inner], wide_keep[inner]

    def first_substep(wide_x):
        mixed_adj = column_solve(wide_x, inv_w, lower_w, factor_w)
        return advect_inner(mixed_adj, wide_east, wide_north) * keep_i

    def second_substep(inner_x):
        mixed_adj = column_solve(inner_x, inv_i, lower_i, factor_i)
        return advect_inner(mixed_adj, east_i, north_i) * keep_factor

    total_steps = NCPL * NSUB
    plane = field_part.shape[1:]
    in_flight = {}
    saved = None
    for block in range((total_steps + SKEW) // NSUB):
        advanced = second_substep(first_substep(widen(field_part, halo)))
        for c, (stage, value) in list(in_flight.items()):
            if stage == 0:
                value, _ = lax.optimization_barrier((value, advanced))
                in_flight[c] = (1, reduce_forcing(value, one_hot))
        step = block * NSUB + NSUB - 1
        if step < SKEW:
            field_part = jnp.where(is_ocean, field_part, advanced)
        else:
            field_part = advanced
        air_done = step + 1
        if air_done <= total_steps and air_done % NSUB == 0:
            in_flight[air_done // NSUB - 1] = (
                0, couple(field_part, weight_table, source_block, peer_count))
        if step == total_steps - 1:
            saved = field_part
        ocean_done = step - SKEW + 1
        if ocean_done >= 1 and ocean_done % NSUB == 0:
            stage, parts = in_flight.pop(ocean_done // NSUB - 1)
            forcing = forcing_field(parts, plane)
            field_part = field_part.at[0].add(
                jnp.where(is_ocean, forcing * ocean_keep, jnp.zeros_like(forcing))
            )
    field_part = jnp.where(is_ocean, field_part, saved)
    return field_part[None]


def solution(mesh):
    in_specs = (
        P("sec", None, "lat", "lon"),
        P("sec", None, "lat", "lon"),
        P("sec", None, "lat", "lon"),
        P("sec", None, "lat", "lon"),
        P("lat", "lon"),
        P("sec", "lat", "lon", None, None, None),
        P("sec", "lat", "lon", None, None),
        P("sec", "lat", "lon", None, None),
        P("sec", "lat", "lon", None),
    )
    out_specs = P("sec", None, "lat", "lon")
    return jax.shard_map(local, mesh=mesh, in_specs=in_specs, out_specs=out_specs, check_vma=False)
```

```python
import jax
import jax.numpy as jnp
from jax import lax
from jax.experimental import pallas as pl
from jax.experimental.pallas import tpu as pltpu
from jax.sharding import PartitionSpec as P

NCPL = 4
NSUB = 2
SKEW = 2


def extended(block, sides, width, periodic):
    for axis, dim in sides:
        count = lax.axis_size(axis)
        forward = [(i, i + 1) for i in range(count - 1)]
        if periodic:
            forward.append((count - 1, 0))
        backward = [(target, source) for source, target in forward]
        low = lax.ppermute(
            lax.slice_in_dim(block, block.shape[dim] - width, None, axis=dim), axis, forward
        )
        high = lax.ppermute(lax.slice_in_dim(block, 0, width, axis=dim), axis, backward)
        block = jnp.concatenate([low, block, high], axis=dim)
    return block


def _factor_kernel(a_ref, inv_ref, b_ref, c_ref):
    lev = a_ref.shape[0]
    prior_c = jnp.zeros(a_ref.shape[1:], jnp.float32)
    zero = jnp.zeros(a_ref.shape[1:], jnp.float32)
    for k in range(lev):
        lower = a_ref[k] if k >= 1 else zero
        upper = a_ref[k + 1] if k + 1 < lev else zero
        centre = 1.0 + lower + upper
        pivot = centre + lower * prior_c
        inv = 1.0 / pivot
        factor = -upper / pivot
        inv_ref[k] = inv
        b_ref[k] = lower * inv
        c_ref[k] = factor
        prior_c = factor


def _solve_kernel(x_ref, inv_ref, b_ref, c_ref, o_ref):
    lev = x_ref.shape[0]

    def down(k, z):
        z = x_ref[k] * inv_ref[k] + b_ref[k] * z
        o_ref[k] = z
        return z

    def up(i, x):
        k = lev - 1 - i
        x = o_ref[k] - c_ref[k] * x
        o_ref[k] = x
        return x

    zero = jnp.zeros(x_ref.shape[1:], jnp.float32)
    lax.fori_loop(0, lev, down, zero, unroll=5)
    lax.fori_loop(0, lev, up, zero, unroll=5)


def factorise(coeff):
    shape = jax.ShapeDtypeStruct(coeff.shape, jnp.float32)
    size = coeff.size
    return pl.pallas_call(
        _factor_kernel,
        out_shape=(shape, shape, shape),
        cost_estimate=pl.CostEstimate(flops=8 * size, bytes_accessed=16 * size, transcendentals=0),
    )(coeff)


def column_solve(right, inv, lower, factor):
    size = right.size
    return pl.pallas_call(
        _solve_kernel,
        out_shape=jax.ShapeDtypeStruct(right.shape, jnp.float32),
        cost_estimate=pl.CostEstimate(flops=6 * size, bytes_accessed=20 * size, transcendentals=0),
    )(right, inv, lower, factor)


def advect(mixed_adj, east_speed, north_speed):
    east_flux = east_speed * mixed_adj
    north_flux = north_speed * mixed_adj
    east_rim = extended(east_flux, (("lon", 2),), 1, True)
    north_rim = extended(north_flux, (("lat", 1),), 1, False)
    east_diff = east_rim[:, :, 2:] - east_rim[:, :, :-2]
    north_diff = north_rim[:, 2:, :] - north_rim[:, :-2, :]
    return mixed_adj + 0.5 * (east_diff + north_diff)


def couple(field_part, weight_table, source_block, peer_count):
    block_cells = weight_table.shape[0]
    capacity = source_block.shape[-1]
    surface = field_part[-1].reshape(-1, block_cells)
    gathered = jnp.take(surface, source_block.reshape(-1), axis=0)
    contribution = jnp.einsum("diz,zi->dz", weight_table, gathered, precision=lax.Precision.HIGHEST)
    lat_count, lon_count = lax.axis_size("lat"), lax.axis_size("lon")
    staged = contribution.reshape(block_cells, lat_count, lon_count, capacity)
    staged = lax.all_to_all(staged, "lon", split_axis=2, concat_axis=2, tiled=True)
    staged = lax.all_to_all(staged, "lat", split_axis=1, concat_axis=1, tiled=True)
    return staged.reshape(block_cells, peer_count, capacity)


def reduce_forcing(received, one_hot):
    block_cells = received.shape[0]
    arrived = received.reshape(block_cells, -1)
    accumulated = jnp.dot(
        arrived, one_hot, precision=lax.Precision.HIGHEST, preferred_element_type=jnp.float32
    )
    section_count = lax.axis_size("sec")
    return [lax.ppermute(accumulated, "sec", [(s, section_count - 1)]) for s in range(section_count - 1)]


def forcing_field(parts, shape):
    total = parts[0]
    for part in parts[1:]:
        total = total + part
    return total.T.reshape(shape)


def local(
    state, mixing, eastward, northward, sea_mask, weights, source_block, dest_block, record_counts
):
    section = lax.axis_index("sec")
    section_count = lax.axis_size("sec")
    is_ocean = section == section_count - 1
    ocean_keep = sea_mask.astype(jnp.float32)
    keep_factor = jnp.where(is_ocean, ocean_keep, jnp.ones_like(ocean_keep))
    field_part = state[0]
    inv, lower, factor = factorise(mixing[0].astype(jnp.float32))
    east_part = eastward[0].astype(jnp.float32)
    north_part = northward[0].astype(jnp.float32)

    weight_table = weights[0, 0, 0].astype(jnp.float32)
    block_count = field_part.shape[1] * field_part.shape[2] // weight_table.shape[0]
    capacity = source_block.shape[-1]
    live_slot = (
        jnp.arange(capacity, dtype=jnp.int32)[None, :] < record_counts[0, 0, 0][:, None]
    ).reshape(-1)
    matches = dest_block.reshape(-1)[:, None] == jnp.arange(block_count, dtype=jnp.int32)[None, :]
    one_hot = jnp.logical_and(matches, live_slot[:, None]).astype(jnp.float32)

    def substep(x):
        mixed_adj = column_solve(x, inv, lower, factor)
        return advect(mixed_adj, east_part, north_part) * keep_factor

    total_steps = NCPL * NSUB
    peer_count = record_counts.shape[-1]
    plane = field_part.shape[1:]
    in_flight = {}
    saved = None
    for step in range(total_steps + SKEW):
        advanced = substep(field_part)
        if step < SKEW:
            field_part = jnp.where(is_ocean, field_part, advanced)
        else:
            field_part = advanced
        for c, (stage, value) in list(in_flight.items()):
            if stage == 0:
                value, _ = lax.optimization_barrier((value, field_part))
                in_flight[c] = (1, reduce_forcing(value, one_hot))
        air_done = step + 1
        if air_done <= total_steps and air_done % NSUB == 0:
            in_flight[air_done // NSUB - 1] = (
                0, couple(field_part, weight_table, source_block, peer_count))
        if step == total_steps - 1:
            saved = field_part
        ocean_done = step - SKEW + 1
        if ocean_done >= 1 and ocean_done % NSUB == 0:
            stage, parts = in_flight.pop(ocean_done // NSUB - 1)
            forcing = forcing_field(parts, plane)
            field_part = field_part.at[0].add(
                jnp.where(is_ocean, forcing * ocean_keep, jnp.zeros_like(forcing))
            )
    field_part = jnp.where(is_ocean, field_part, saved)
    return field_part[None]


def solution(mesh):
    in_specs = (
        P("sec", None, "lat", "lon"),
        P("sec", None, "lat", "lon"),
        P("sec", None, "lat", "lon"),
        P("sec", None, "lat", "lon"),
        P("lat", "lon"),
        P("sec", "lat", "lon", None, None, None),
        P("sec", "lat", "lon", None, None),
        P("sec", "lat", "lon", None, None),
        P("sec", "lat", "lon", None),
    )
    out_specs = P("sec", None, "lat", "lon")
    return jax.shard_map(local, mesh=mesh, in_specs=in_specs, out_specs=out_specs, check_vma=False)
```

```python
import jax
import jax.numpy as jnp
from jax import lax
from jax.experimental import pallas as pl
from jax.experimental.pallas import tpu as pltpu
from jax.sharding import PartitionSpec as P

NCPL = 4
NSUB = 2
SKEW = 1


def extended(block, sides, width, periodic):
    for axis, dim in sides:
        count = lax.axis_size(axis)
        forward = [(i, i + 1) for i in range(count - 1)]
        if periodic:
            forward.append((count - 1, 0))
        backward = [(target, source) for source, target in forward]
        low = lax.ppermute(
            lax.slice_in_dim(block, block.shape[dim] - width, None, axis=dim), axis, forward
        )
        high = lax.ppermute(lax.slice_in_dim(block, 0, width, axis=dim), axis, backward)
        block = jnp.concatenate([low, block, high], axis=dim)
    return block


def _factor_kernel(a_ref, inv_ref, b_ref, c_ref):
    lev = a_ref.shape[0]
    prior_c = jnp.zeros(a_ref.shape[1:], jnp.float32)
    zero = jnp.zeros(a_ref.shape[1:], jnp.float32)
    for k in range(lev):
        lower = a_ref[k] if k >= 1 else zero
        upper = a_ref[k + 1] if k + 1 < lev else zero
        centre = 1.0 + lower + upper
        pivot = centre + lower * prior_c
        inv = 1.0 / pivot
        factor = -upper / pivot
        inv_ref[k] = inv
        b_ref[k] = lower * inv
        c_ref[k] = factor
        prior_c = factor


def _solve_kernel(x_ref, inv_ref, b_ref, c_ref, o_ref):
    lev = x_ref.shape[0]

    def down(k, z):
        z = x_ref[k] * inv_ref[k] + b_ref[k] * z
        o_ref[k] = z
        return z

    def up(i, x):
        k = lev - 1 - i
        x = o_ref[k] - c_ref[k] * x
        o_ref[k] = x
        return x

    zero = jnp.zeros(x_ref.shape[1:], jnp.float32)
    lax.fori_loop(0, lev, down, zero, unroll=5)
    lax.fori_loop(0, lev, up, zero, unroll=5)


def factorise(coeff):
    shape = jax.ShapeDtypeStruct(coeff.shape, jnp.float32)
    size = coeff.size
    return pl.pallas_call(
        _factor_kernel,
        out_shape=(shape, shape, shape),
        cost_estimate=pl.CostEstimate(flops=8 * size, bytes_accessed=16 * size, transcendentals=0),
    )(coeff)


def column_solve(right, inv, lower, factor):
    size = right.size
    return pl.pallas_call(
        _solve_kernel,
        out_shape=jax.ShapeDtypeStruct(right.shape, jnp.float32),
        cost_estimate=pl.CostEstimate(flops=6 * size, bytes_accessed=20 * size, transcendentals=0),
    )(right, inv, lower, factor)


def advect(mixed_adj, east_speed, north_speed):
    east_flux = east_speed * mixed_adj
    north_flux = north_speed * mixed_adj
    east_rim = extended(east_flux, (("lon", 2),), 1, True)
    north_rim = extended(north_flux, (("lat", 1),), 1, False)
    east_diff = east_rim[:, :, 2:] - east_rim[:, :, :-2]
    north_diff = north_rim[:, 2:, :] - north_rim[:, :-2, :]
    return mixed_adj + 0.5 * (east_diff + north_diff)


def couple(field_part, weight_table, source_block, peer_count):
    block_cells = weight_table.shape[0]
    capacity = source_block.shape[-1]
    surface = field_part[-1].reshape(-1, block_cells)
    gathered = jnp.take(surface, source_block.reshape(-1), axis=0)
    contribution = jnp.einsum("diz,zi->dz", weight_table, gathered, precision=lax.Precision.HIGHEST)
    lat_count, lon_count = lax.axis_size("lat"), lax.axis_size("lon")
    staged = contribution.reshape(block_cells, lat_count, lon_count, capacity)
    staged = lax.all_to_all(staged, "lon", split_axis=2, concat_axis=2, tiled=True)
    staged = lax.all_to_all(staged, "lat", split_axis=1, concat_axis=1, tiled=True)
    return staged.reshape(block_cells, peer_count, capacity)


def reduce_forcing(received, one_hot):
    block_cells = received.shape[0]
    arrived = received.reshape(block_cells, -1)
    accumulated = jnp.dot(
        arrived, one_hot, precision=lax.Precision.HIGHEST, preferred_element_type=jnp.float32
    )
    section_count = lax.axis_size("sec")
    return [lax.ppermute(accumulated, "sec", [(s, section_count - 1)]) for s in range(section_count - 1)]


def forcing_field(parts, shape):
    total = parts[0]
    for part in parts[1:]:
        total = total + part
    return total.T.reshape(shape)


def local(
    state, mixing, eastward, northward, sea_mask, weights, source_block, dest_block, record_counts
):
    section = lax.axis_index("sec")
    section_count = lax.axis_size("sec")
    is_ocean = section == section_count - 1
    ocean_keep = sea_mask.astype(jnp.float32)
    keep_factor = jnp.where(is_ocean, ocean_keep, jnp.ones_like(ocean_keep))
    field_part = state[0]
    inv, lower, factor = factorise(mixing[0].astype(jnp.float32))
    east_part = eastward[0].astype(jnp.float32)
    north_part = northward[0].astype(jnp.float32)

    weight_table = weights[0, 0, 0].astype(jnp.float32)
    block_count = field_part.shape[1] * field_part.shape[2] // weight_table.shape[0]
    capacity = source_block.shape[-1]
    live_slot = (
        jnp.arange(capacity, dtype=jnp.int32)[None, :] < record_counts[0, 0, 0][:, None]
    ).reshape(-1)
    matches = dest_block.reshape(-1)[:, None] == jnp.arange(block_count, dtype=jnp.int32)[None, :]
    one_hot = jnp.logical_and(matches, live_slot[:, None]).astype(jnp.float32)

    def substep(x):
        mixed_adj = column_solve(x, inv, lower, factor)
        return advect(mixed_adj, east_part, north_part) * keep_factor

    total_steps = NCPL * NSUB
    peer_count = record_counts.shape[-1]
    plane = field_part.shape[1:]
    in_flight = {}
    saved = None
    for step in range(total_steps + SKEW):
        advanced = substep(field_part)
        if step < SKEW:
            field_part = jnp.where(is_ocean, field_part, advanced)
        else:
            field_part = advanced
        for c, (stage, value) in list(in_flight.items()):
            if stage == 0:
                value, _ = lax.optimization_barrier((value, field_part))
                in_flight[c] = (1, reduce_forcing(value, one_hot))
        air_done = step + 1
        if air_done <= total_steps and air_done % NSUB == 0:
            in_flight[air_done // NSUB - 1] = (
                0, couple(field_part, weight_table, source_block, peer_count))
        if step == total_steps - 1:
            saved = field_part
        ocean_done = step - SKEW + 1
        if ocean_done >= 1 and ocean_done % NSUB == 0:
            stage, parts = in_flight.pop(ocean_done // NSUB - 1)
            forcing = forcing_field(parts, plane)
            field_part = field_part.at[0].add(
                jnp.where(is_ocean, forcing * ocean_keep, jnp.zeros_like(forcing))
            )
    field_part = jnp.where(is_ocean, field_part, saved)
    return field_part[None]


def solution(mesh):
    in_specs = (
        P("sec", None, "lat", "lon"),
        P("sec", None, "lat", "lon"),
        P("sec", None, "lat", "lon"),
        P("sec", None, "lat", "lon"),
        P("lat", "lon"),
        P("sec", "lat", "lon", None, None, None),
        P("sec", "lat", "lon", None, None),
        P("sec", "lat", "lon", None, None),
        P("sec", "lat", "lon", None),
    )
    out_specs = P("sec", None, "lat", "lon")
    return jax.shard_map(local, mesh=mesh, in_specs=in_specs, out_specs=out_specs, check_vma=False)
```

```python
import jax
import jax.numpy as jnp
from jax import lax
from jax.experimental import pallas as pl
from jax.experimental.pallas import tpu as pltpu
from jax.sharding import PartitionSpec as P

NCPL = 4
NSUB = 2
SKEW = 2


def extended(block, sides, width, periodic):
    for axis, dim in sides:
        count = lax.axis_size(axis)
        forward = [(i, i + 1) for i in range(count - 1)]
        if periodic:
            forward.append((count - 1, 0))
        backward = [(target, source) for source, target in forward]
        low = lax.ppermute(
            lax.slice_in_dim(block, block.shape[dim] - width, None, axis=dim), axis, forward
        )
        high = lax.ppermute(lax.slice_in_dim(block, 0, width, axis=dim), axis, backward)
        block = jnp.concatenate([low, block, high], axis=dim)
    return block


def _factor_kernel(a_ref, inv_ref, b_ref, c_ref):
    lev = a_ref.shape[0]
    prior_c = jnp.zeros(a_ref.shape[1:], jnp.float32)
    zero = jnp.zeros(a_ref.shape[1:], jnp.float32)
    for k in range(lev):
        lower = a_ref[k] if k >= 1 else zero
        upper = a_ref[k + 1] if k + 1 < lev else zero
        centre = 1.0 + lower + upper
        pivot = centre + lower * prior_c
        inv = 1.0 / pivot
        factor = -upper / pivot
        inv_ref[k] = inv
        b_ref[k] = lower * inv
        c_ref[k] = factor
        prior_c = factor


def _solve_kernel(x_ref, inv_ref, b_ref, c_ref, east_ref, north_ref, o_ref, e_ref, n_ref):
    lev = x_ref.shape[0]

    def down(k, z):
        z = x_ref[k] * inv_ref[k] + b_ref[k] * z
        o_ref[k] = z
        return z

    def up(i, x):
        k = lev - 1 - i
        x = o_ref[k] - c_ref[k] * x
        o_ref[k] = x
        e_ref[k] = east_ref[k] * x
        n_ref[k] = north_ref[k] * x
        return x

    zero = jnp.zeros(x_ref.shape[1:], jnp.float32)
    lax.fori_loop(0, lev, down, zero, unroll=5)
    lax.fori_loop(0, lev, up, zero, unroll=5)


def factorise(coeff):
    shape = jax.ShapeDtypeStruct(coeff.shape, jnp.float32)
    size = coeff.size
    return pl.pallas_call(
        _factor_kernel,
        out_shape=(shape, shape, shape),
        cost_estimate=pl.CostEstimate(flops=8 * size, bytes_accessed=16 * size, transcendentals=0),
    )(coeff)


def column_solve(right, inv, lower, factor, east_speed, north_speed):
    size = right.size
    shape = jax.ShapeDtypeStruct(right.shape, jnp.float32)
    return pl.pallas_call(
        _solve_kernel,
        out_shape=(shape, shape, shape),
        cost_estimate=pl.CostEstimate(flops=8 * size, bytes_accessed=36 * size, transcendentals=0),
    )(right, inv, lower, factor, east_speed, north_speed)


def advect(mixed_adj, east_flux, north_flux):
    east_rim = extended(east_flux, (("lon", 2),), 1, True)
    north_rim = extended(north_flux, (("lat", 1),), 1, False)
    east_diff = east_rim[:, :, 2:] - east_rim[:, :, :-2]
    north_diff = north_rim[:, 2:, :] - north_rim[:, :-2, :]
    return mixed_adj + 0.5 * (east_diff + north_diff)


def couple(field_part, weight_table, source_block, peer_count):
    block_cells = weight_table.shape[0]
    capacity = source_block.shape[-1]
    surface = field_part[-1].reshape(-1, block_cells)
    gathered = jnp.take(surface, source_block.reshape(-1), axis=0)
    contribution = jnp.einsum("diz,zi->dz", weight_table, gathered, precision=lax.Precision.HIGHEST)
    lat_count, lon_count = lax.axis_size("lat"), lax.axis_size("lon")
    staged = contribution.reshape(block_cells, lat_count, lon_count, capacity)
    staged = lax.all_to_all(staged, "lon", split_axis=2, concat_axis=2, tiled=True)
    staged = lax.all_to_all(staged, "lat", split_axis=1, concat_axis=1, tiled=True)
    return staged.reshape(block_cells, peer_count, capacity)


def reduce_forcing(received, one_hot):
    block_cells = received.shape[0]
    arrived = received.reshape(block_cells, -1)
    accumulated = jnp.dot(
        arrived, one_hot, precision=lax.Precision.HIGHEST, preferred_element_type=jnp.float32
    )
    section_count = lax.axis_size("sec")
    return [lax.ppermute(accumulated, "sec", [(s, section_count - 1)]) for s in range(section_count - 1)]


def forcing_field(parts, shape):
    total = parts[0]
    for part in parts[1:]:
        total = total + part
    return total.T.reshape(shape)


def local(
    state, mixing, eastward, northward, sea_mask, weights, source_block, dest_block, record_counts
):
    section = lax.axis_index("sec")
    section_count = lax.axis_size("sec")
    is_ocean = section == section_count - 1
    ocean_keep = sea_mask.astype(jnp.float32)
    keep_factor = jnp.where(is_ocean, ocean_keep, jnp.ones_like(ocean_keep))
    field_part = state[0]
    inv, lower, factor = factorise(mixing[0].astype(jnp.float32))
    east_part = eastward[0].astype(jnp.float32)
    north_part = northward[0].astype(jnp.float32)

    weight_table = weights[0, 0, 0].astype(jnp.float32)
    block_count = field_part.shape[1] * field_part.shape[2] // weight_table.shape[0]
    capacity = source_block.shape[-1]
    live_slot = (
        jnp.arange(capacity, dtype=jnp.int32)[None, :] < record_counts[0, 0, 0][:, None]
    ).reshape(-1)
    matches = dest_block.reshape(-1)[:, None] == jnp.arange(block_count, dtype=jnp.int32)[None, :]
    one_hot = jnp.logical_and(matches, live_slot[:, None]).astype(jnp.float32)

    def substep(x):
        mixed_adj, east_flux, north_flux = column_solve(x, inv, lower, factor, east_part, north_part)
        return advect(mixed_adj, east_flux, north_flux) * keep_factor

    total_steps = NCPL * NSUB
    peer_count = record_counts.shape[-1]
    plane = field_part.shape[1:]
    in_flight = {}
    saved = None
    for step in range(total_steps + SKEW):
        advanced = substep(field_part)
        if step < SKEW:
            field_part = jnp.where(is_ocean, field_part, advanced)
        else:
            field_part = advanced
        for c, (stage, value) in list(in_flight.items()):
            if stage == 0:
                value, _ = lax.optimization_barrier((value, field_part))
                in_flight[c] = (1, reduce_forcing(value, one_hot))
        air_done = step + 1
        if air_done <= total_steps and air_done % NSUB == 0:
            in_flight[air_done // NSUB - 1] = (
                0, couple(field_part, weight_table, source_block, peer_count))
        if step == total_steps - 1:
            saved = field_part
        ocean_done = step - SKEW + 1
        if ocean_done >= 1 and ocean_done % NSUB == 0:
            stage, parts = in_flight.pop(ocean_done // NSUB - 1)
            forcing = forcing_field(parts, plane)
            field_part = field_part.at[0].add(
                jnp.where(is_ocean, forcing * ocean_keep, jnp.zeros_like(forcing))
            )
    field_part = jnp.where(is_ocean, field_part, saved)
    return field_part[None]


def solution(mesh):
    in_specs = (
        P("sec", None, "lat", "lon"),
        P("sec", None, "lat", "lon"),
        P("sec", None, "lat", "lon"),
        P("sec", None, "lat", "lon"),
        P("lat", "lon"),
        P("sec", "lat", "lon", None, None, None),
        P("sec", "lat", "lon", None, None),
        P("sec", "lat", "lon", None, None),
        P("sec", "lat", "lon", None),
    )
    out_specs = P("sec", None, "lat", "lon")
    return jax.shard_map(local, mesh=mesh, in_specs=in_specs, out_specs=out_specs, check_vma=False)
```

```python
import jax
import jax.numpy as jnp
from jax import lax
from jax.experimental import pallas as pl
from jax.experimental.pallas import tpu as pltpu
from jax.sharding import PartitionSpec as P

NCPL = 4
NSUB = 2
SKEW = 2


def extended(block, sides, width, periodic):
    for axis, dim in sides:
        count = lax.axis_size(axis)
        forward = [(i, i + 1) for i in range(count - 1)]
        if periodic:
            forward.append((count - 1, 0))
        backward = [(target, source) for source, target in forward]
        low = lax.ppermute(
            lax.slice_in_dim(block, block.shape[dim] - width, None, axis=dim), axis, forward
        )
        high = lax.ppermute(lax.slice_in_dim(block, 0, width, axis=dim), axis, backward)
        block = jnp.concatenate([low, block, high], axis=dim)
    return block


def _factor_kernel(a_ref, inv_ref, b_ref, c_ref):
    lev = a_ref.shape[0]
    prior_c = jnp.zeros(a_ref.shape[1:], jnp.float32)
    zero = jnp.zeros(a_ref.shape[1:], jnp.float32)
    for k in range(lev):
        lower = a_ref[k] if k >= 1 else zero
        upper = a_ref[k + 1] if k + 1 < lev else zero
        centre = 1.0 + lower + upper
        pivot = centre + lower * prior_c
        inv = 1.0 / pivot
        factor = -upper / pivot
        inv_ref[k] = inv
        b_ref[k] = lower * inv
        c_ref[k] = factor
        prior_c = factor


def _solve_kernel(x_ref, inv_ref, b_ref, c_ref, o_ref):
    lev = x_ref.shape[0]

    def down(k, z):
        z = x_ref[k] * inv_ref[k] + b_ref[k] * z
        o_ref[k] = z
        return z

    def up(i, x):
        k = lev - 1 - i
        x = o_ref[k] - c_ref[k] * x
        o_ref[k] = x
        return x

    zero = jnp.zeros(x_ref.shape[1:], jnp.float32)
    lax.fori_loop(0, lev, down, zero, unroll=5)
    lax.fori_loop(0, lev, up, zero, unroll=5)


def factorise(coeff):
    shape = jax.ShapeDtypeStruct(coeff.shape, jnp.float32)
    size = coeff.size
    return pl.pallas_call(
        _factor_kernel,
        out_shape=(shape, shape, shape),
        cost_estimate=pl.CostEstimate(flops=8 * size, bytes_accessed=16 * size, transcendentals=0),
    )(coeff)


def column_solve(right, inv, lower, factor):
    size = right.size
    return pl.pallas_call(
        _solve_kernel,
        out_shape=jax.ShapeDtypeStruct(right.shape, jnp.float32),
        cost_estimate=pl.CostEstimate(flops=6 * size, bytes_accessed=20 * size, transcendentals=0),
    )(right, inv, lower, factor)


def advect(mixed_adj, east_speed, north_speed):
    east_flux = east_speed * mixed_adj
    north_flux = north_speed * mixed_adj
    east_rim = extended(east_flux, (("lon", 2),), 1, True)
    north_rim = extended(north_flux, (("lat", 1),), 1, False)
    east_diff = east_rim[:, :, 2:] - east_rim[:, :, :-2]
    north_diff = north_rim[:, 2:, :] - north_rim[:, :-2, :]
    return mixed_adj + 0.5 * (east_diff + north_diff)


def section_exchange(values, axis):
    lat_count, lon_count = lax.axis_size("lat"), lax.axis_size("lon")
    shape = values.shape
    staged = values.reshape(shape[:axis] + (lat_count, lon_count) + shape[axis + 1 :])
    staged = lax.all_to_all(staged, "lon", split_axis=axis + 1, concat_axis=axis + 1, tiled=True)
    staged = lax.all_to_all(staged, "lat", split_axis=axis, concat_axis=axis, tiled=True)
    return staged.reshape(shape)


def couple(field_part, weight_table, source_block, one_hot_out):
    block_cells = weight_table.shape[0]
    peer_count, capacity = one_hot_out.shape[:2]
    surface = field_part[-1].reshape(-1, block_cells)
    gathered = jnp.take(surface, source_block.reshape(-1), axis=0)
    contribution = jnp.einsum("diz,zi->dz", weight_table, gathered, precision=lax.Precision.HIGHEST)
    partial = jnp.einsum(
        "drj,rjb->rdb",
        contribution.reshape(block_cells, peer_count, capacity),
        one_hot_out,
        precision=lax.Precision.HIGHEST,
    )
    return lax.psum_scatter(partial, ("lat", "lon"), scatter_dimension=0, tiled=True)


def reduce_forcing(received, one_hot):
    accumulated = received[0]
    section_count = lax.axis_size("sec")
    return [lax.ppermute(accumulated, "sec", [(s, section_count - 1)]) for s in range(section_count - 1)]


def forcing_field(parts, shape):
    total = parts[0]
    for part in parts[1:]:
        total = total + part
    return total.T.reshape(shape)


def local(
    state, mixing, eastward, northward, sea_mask, weights, source_block, dest_block, record_counts
):
    section = lax.axis_index("sec")
    section_count = lax.axis_size("sec")
    is_ocean = section == section_count - 1
    ocean_keep = sea_mask.astype(jnp.float32)
    keep_factor = jnp.where(is_ocean, ocean_keep, jnp.ones_like(ocean_keep))
    field_part = state[0]
    inv, lower, factor = factorise(mixing[0].astype(jnp.float32))
    east_part = eastward[0].astype(jnp.float32)
    north_part = northward[0].astype(jnp.float32)

    weight_table = weights[0, 0, 0].astype(jnp.float32)
    block_count = field_part.shape[1] * field_part.shape[2] // weight_table.shape[0]
    capacity = source_block.shape[-1]
    live_slot = jnp.arange(capacity, dtype=jnp.int32)[None, :] < record_counts[0, 0, 0][:, None]
    dest_out = section_exchange(jnp.where(live_slot, dest_block[0, 0, 0], -1), 0)
    one_hot_out = (
        dest_out[:, :, None] == jnp.arange(block_count, dtype=jnp.int32)[None, None, :]
    ).astype(jnp.float32)
    one_hot = None

    def substep(x):
        mixed_adj = column_solve(x, inv, lower, factor)
        return advect(mixed_adj, east_part, north_part) * keep_factor

    total_steps = NCPL * NSUB
    peer_count = record_counts.shape[-1]
    plane = field_part.shape[1:]
    in_flight = {}
    saved = None
    for step in range(total_steps + SKEW):
        advanced = substep(field_part)
        if step < SKEW:
            field_part = jnp.where(is_ocean, field_part, advanced)
        else:
            field_part = advanced
        for c, (stage, value) in list(in_flight.items()):
            if stage == 0:
                value, _ = lax.optimization_barrier((value, field_part))
                in_flight[c] = (1, reduce_forcing(value, one_hot))
        air_done = step + 1
        if air_done <= total_steps and air_done % NSUB == 0:
            in_flight[air_done // NSUB - 1] = (
                0, couple(field_part, weight_table, source_block, one_hot_out))
        if step == total_steps - 1:
            saved = field_part
        ocean_done = step - SKEW + 1
        if ocean_done >= 1 and ocean_done % NSUB == 0:
            stage, parts = in_flight.pop(ocean_done // NSUB - 1)
            forcing = forcing_field(parts, plane)
            field_part = field_part.at[0].add(
                jnp.where(is_ocean, forcing * ocean_keep, jnp.zeros_like(forcing))
            )
    field_part = jnp.where(is_ocean, field_part, saved)
    return field_part[None]


def solution(mesh):
    in_specs = (
        P("sec", None, "lat", "lon"),
        P("sec", None, "lat", "lon"),
        P("sec", None, "lat", "lon"),
        P("sec", None, "lat", "lon"),
        P("lat", "lon"),
        P("sec", "lat", "lon", None, None, None),
        P("sec", "lat", "lon", None, None),
        P("sec", "lat", "lon", None, None),
        P("sec", "lat", "lon", None),
    )
    out_specs = P("sec", None, "lat", "lon")
    return jax.shard_map(local, mesh=mesh, in_specs=in_specs, out_specs=out_specs, check_vma=False)
```

```python
import jax
import jax.numpy as jnp
from jax import lax
from jax.experimental import pallas as pl
from jax.experimental.pallas import tpu as pltpu
from jax.sharding import PartitionSpec as P

NCPL = 4
NSUB = 2
SKEW = 2


def extended(block, sides, width, periodic):
    for axis, dim in sides:
        count = lax.axis_size(axis)
        forward = [(i, i + 1) for i in range(count - 1)]
        if periodic:
            forward.append((count - 1, 0))
        backward = [(target, source) for source, target in forward]
        low = lax.ppermute(
            lax.slice_in_dim(block, block.shape[dim] - width, None, axis=dim), axis, forward
        )
        high = lax.ppermute(lax.slice_in_dim(block, 0, width, axis=dim), axis, backward)
        block = jnp.concatenate([low, block, high], axis=dim)
    return block


def _factor_kernel(a_ref, inv_ref, b_ref, c_ref):
    lev = a_ref.shape[0]
    prior_c = jnp.zeros(a_ref.shape[1:], jnp.float32)
    zero = jnp.zeros(a_ref.shape[1:], jnp.float32)
    for k in range(lev):
        lower = a_ref[k] if k >= 1 else zero
        upper = a_ref[k + 1] if k + 1 < lev else zero
        centre = 1.0 + lower + upper
        pivot = centre + lower * prior_c
        inv = 1.0 / pivot
        factor = -upper / pivot
        inv_ref[k] = inv
        b_ref[k] = lower * inv
        c_ref[k] = factor
        prior_c = factor


def _solve_kernel(x_ref, inv_ref, b_ref, c_ref, o_ref):
    lev = x_ref.shape[0]

    def down(k, z):
        z = x_ref[k] * inv_ref[k] + b_ref[k] * z
        o_ref[k] = z
        return z

    def up(i, x):
        k = lev - 1 - i
        x = o_ref[k] - c_ref[k] * x
        o_ref[k] = x
        return x

    zero = jnp.zeros(x_ref.shape[1:], jnp.float32)
    lax.fori_loop(0, lev, down, zero, unroll=5)
    lax.fori_loop(0, lev, up, zero, unroll=5)


def factorise(coeff):
    shape = jax.ShapeDtypeStruct(coeff.shape, jnp.float32)
    size = coeff.size
    return pl.pallas_call(
        _factor_kernel,
        out_shape=(shape, shape, shape),
        cost_estimate=pl.CostEstimate(flops=8 * size, bytes_accessed=16 * size, transcendentals=0),
    )(coeff)


def column_solve(right, inv, lower, factor):
    size = right.size
    return pl.pallas_call(
        _solve_kernel,
        out_shape=jax.ShapeDtypeStruct(right.shape, jnp.float32),
        cost_estimate=pl.CostEstimate(flops=6 * size, bytes_accessed=20 * size, transcendentals=0),
    )(right, inv, lower, factor)


def advect(mixed_adj, east_speed, north_speed):
    east_flux = east_speed * mixed_adj
    north_flux = north_speed * mixed_adj
    east_rim = extended(east_flux, (("lon", 2),), 1, True)
    north_rim = extended(north_flux, (("lat", 1),), 1, False)
    east_diff = east_rim[:, :, 2:] - east_rim[:, :, :-2]
    north_diff = north_rim[:, 2:, :] - north_rim[:, :-2, :]
    return mixed_adj + 0.5 * (east_diff + north_diff)


def couple(field_part, weight_table, source_block, peer_count):
    block_cells = weight_table.shape[0]
    capacity = source_block.shape[-1]
    surface = field_part[-1].reshape(-1, block_cells)
    gathered = jnp.take(surface, source_block.reshape(-1), axis=0)
    contribution = jnp.einsum("diz,zi->dz", weight_table, gathered, precision=lax.Precision.HIGHEST)
    lat_count, lon_count = lax.axis_size("lat"), lax.axis_size("lon")
    staged = contribution.reshape(block_cells, lat_count, lon_count, capacity)
    staged = lax.all_to_all(staged, "lat", split_axis=1, concat_axis=1, tiled=True)
    staged = lax.all_to_all(staged, "lon", split_axis=2, concat_axis=2, tiled=True)
    return staged.reshape(block_cells, peer_count, capacity)


def reduce_forcing(received, one_hot):
    block_cells = received.shape[0]
    arrived = received.reshape(block_cells, -1)
    accumulated = jnp.dot(
        arrived, one_hot, precision=lax.Precision.HIGHEST, preferred_element_type=jnp.float32
    )
    section_count = lax.axis_size("sec")
    return [lax.ppermute(accumulated, "sec", [(s, section_count - 1)]) for s in range(section_count - 1)]


def forcing_field(parts, shape):
    total = parts[0]
    for part in parts[1:]:
        total = total + part
    return total.T.reshape(shape)


def local(
    state, mixing, eastward, northward, sea_mask, weights, source_block, dest_block, record_counts
):
    section = lax.axis_index("sec")
    section_count = lax.axis_size("sec")
    is_ocean = section == section_count - 1
    ocean_keep = sea_mask.astype(jnp.float32)
    keep_factor = jnp.where(is_ocean, ocean_keep, jnp.ones_like(ocean_keep))
    field_part = state[0]
    inv, lower, factor = factorise(mixing[0].astype(jnp.float32))
    east_part = eastward[0].astype(jnp.float32)
    north_part = northward[0].astype(jnp.float32)

    weight_table = weights[0, 0, 0].astype(jnp.float32)
    block_count = field_part.shape[1] * field_part.shape[2] // weight_table.shape[0]
    capacity = source_block.shape[-1]
    live_slot = (
        jnp.arange(capacity, dtype=jnp.int32)[None, :] < record_counts[0, 0, 0][:, None]
    ).reshape(-1)
    matches = dest_block.reshape(-1)[:, None] == jnp.arange(block_count, dtype=jnp.int32)[None, :]
    one_hot = jnp.logical_and(matches, live_slot[:, None]).astype(jnp.float32)

    def substep(x):
        mixed_adj = column_solve(x, inv, lower, factor)
        return advect(mixed_adj, east_part, north_part) * keep_factor

    total_steps = NCPL * NSUB
    peer_count = record_counts.shape[-1]
    plane = field_part.shape[1:]
    in_flight = {}
    saved = None
    for step in range(total_steps + SKEW):
        advanced = substep(field_part)
        if step < SKEW:
            field_part = jnp.where(is_ocean, field_part, advanced)
        else:
            field_part = advanced
        for c, (stage, value) in list(in_flight.items()):
            if stage == 0:
                value, _ = lax.optimization_barrier((value, field_part))
                in_flight[c] = (1, reduce_forcing(value, one_hot))
        air_done = step + 1
        if air_done <= total_steps and air_done % NSUB == 0:
            in_flight[air_done // NSUB - 1] = (
                0, couple(field_part, weight_table, source_block, peer_count))
        if step == total_steps - 1:
            saved = field_part
        ocean_done = step - SKEW + 1
        if ocean_done >= 1 and ocean_done % NSUB == 0:
            stage, parts = in_flight.pop(ocean_done // NSUB - 1)
            forcing = forcing_field(parts, plane)
            field_part = field_part.at[0].add(
                jnp.where(is_ocean, forcing * ocean_keep, jnp.zeros_like(forcing))
            )
    field_part = jnp.where(is_ocean, field_part, saved)
    return field_part[None]


def solution(mesh):
    in_specs = (
        P("sec", None, "lat", "lon"),
        P("sec", None, "lat", "lon"),
        P("sec", None, "lat", "lon"),
        P("sec", None, "lat", "lon"),
        P("lat", "lon"),
        P("sec", "lat", "lon", None, None, None),
        P("sec", "lat", "lon", None, None),
        P("sec", "lat", "lon", None, None),
        P("sec", "lat", "lon", None),
    )
    out_specs = P("sec", None, "lat", "lon")
    return jax.shard_map(local, mesh=mesh, in_specs=in_specs, out_specs=out_specs, check_vma=False)
```

```python
import jax
import jax.numpy as jnp
from jax import lax
from jax.experimental import pallas as pl
from jax.experimental.pallas import tpu as pltpu
from jax.sharding import PartitionSpec as P

NCPL = 4
NSUB = 2
SKEW = 2


def extended(block, sides, width, periodic):
    for axis, dim in sides:
        count = lax.axis_size(axis)
        forward = [(i, i + 1) for i in range(count - 1)]
        if periodic:
            forward.append((count - 1, 0))
        backward = [(target, source) for source, target in forward]
        low = lax.ppermute(
            lax.slice_in_dim(block, block.shape[dim] - width, None, axis=dim), axis, forward
        )
        high = lax.ppermute(lax.slice_in_dim(block, 0, width, axis=dim), axis, backward)
        block = jnp.concatenate([low, block, high], axis=dim)
    return block


def _factor_kernel(a_ref, inv_ref, b_ref, c_ref):
    lev = a_ref.shape[0]
    zero = jnp.zeros(a_ref.shape[1:], jnp.float32)

    def level(k, prior_c):
        lower = jnp.where(k >= 1, a_ref[k], zero)
        upper = jnp.where(k + 1 < lev, a_ref[jnp.minimum(k + 1, lev - 1)], zero)
        centre = 1.0 + lower + upper
        pivot = centre + lower * prior_c
        inv = 1.0 / pivot
        factor = -upper / pivot
        inv_ref[k] = inv
        b_ref[k] = lower * inv
        c_ref[k] = factor
        return factor

    lax.fori_loop(0, lev, level, zero, unroll=5)


def _solve_kernel(x_ref, inv_ref, b_ref, c_ref, o_ref):
    lev = x_ref.shape[0]

    def down(k, z):
        z = x_ref[k] * inv_ref[k] + b_ref[k] * z
        o_ref[k] = z
        return z

    def up(i, x):
        k = lev - 1 - i
        x = o_ref[k] - c_ref[k] * x
        o_ref[k] = x
        return x

    zero = jnp.zeros(x_ref.shape[1:], jnp.float32)
    lax.fori_loop(0, lev, down, zero, unroll=15)
    lax.fori_loop(0, lev, up, zero, unroll=15)


def factorise(coeff):
    shape = jax.ShapeDtypeStruct(coeff.shape, jnp.float32)
    size = coeff.size
    return pl.pallas_call(
        _factor_kernel,
        out_shape=(shape, shape, shape),
        cost_estimate=pl.CostEstimate(flops=8 * size, bytes_accessed=16 * size, transcendentals=0),
    )(coeff)


def column_solve(right, inv, lower, factor):
    size = right.size
    return pl.pallas_call(
        _solve_kernel,
        out_shape=jax.ShapeDtypeStruct(right.shape, jnp.float32),
        cost_estimate=pl.CostEstimate(flops=6 * size, bytes_accessed=20 * size, transcendentals=0),
    )(right, inv, lower, factor)


def advect(mixed_adj, east_speed, north_speed):
    east_flux = east_speed * mixed_adj
    north_flux = north_speed * mixed_adj
    east_rim = extended(east_flux, (("lon", 2),), 1, True)
    north_rim = extended(north_flux, (("lat", 1),), 1, False)
    east_diff = east_rim[:, :, 2:] - east_rim[:, :, :-2]
    north_diff = north_rim[:, 2:, :] - north_rim[:, :-2, :]
    return mixed_adj + 0.5 * (east_diff + north_diff)


def couple(field_part, weight_table, source_block, peer_count):
    block_cells = weight_table.shape[0]
    capacity = source_block.shape[-1]
    surface = field_part[-1].reshape(-1, block_cells)
    gathered = jnp.take(surface, source_block.reshape(-1), axis=0)
    contribution = jnp.einsum("diz,zi->dz", weight_table, gathered, precision=lax.Precision.HIGHEST)
    lat_count, lon_count = lax.axis_size("lat"), lax.axis_size("lon")
    staged = contribution.reshape(block_cells, lat_count, lon_count, capacity)
    staged = lax.all_to_all(staged, "lon", split_axis=2, concat_axis=2, tiled=True)
    staged = lax.all_to_all(staged, "lat", split_axis=1, concat_axis=1, tiled=True)
    return staged.reshape(block_cells, peer_count, capacity)


def reduce_forcing(received, one_hot):
    block_cells = received.shape[0]
    arrived = received.reshape(block_cells, -1)
    accumulated = jnp.dot(
        arrived, one_hot, precision=lax.Precision.HIGHEST, preferred_element_type=jnp.float32
    )
    section_count = lax.axis_size("sec")
    return [lax.ppermute(accumulated, "sec", [(s, section_count - 1)]) for s in range(section_count - 1)]


def forcing_field(parts, shape):
    total = parts[0]
    for part in parts[1:]:
        total = total + part
    return total.T.reshape(shape)


def local(
    state, mixing, eastward, northward, sea_mask, weights, source_block, dest_block, record_counts
):
    section = lax.axis_index("sec")
    section_count = lax.axis_size("sec")
    is_ocean = section == section_count - 1
    ocean_keep = sea_mask.astype(jnp.float32)
    keep_factor = jnp.where(is_ocean, ocean_keep, jnp.ones_like(ocean_keep))
    field_part = state[0]
    inv, lower, factor = factorise(mixing[0].astype(jnp.float32))
    east_part = eastward[0].astype(jnp.float32)
    north_part = northward[0].astype(jnp.float32)

    weight_table = weights[0, 0, 0].astype(jnp.float32)
    block_count = field_part.shape[1] * field_part.shape[2] // weight_table.shape[0]
    capacity = source_block.shape[-1]
    live_slot = (
        jnp.arange(capacity, dtype=jnp.int32)[None, :] < record_counts[0, 0, 0][:, None]
    ).reshape(-1)
    matches = dest_block.reshape(-1)[:, None] == jnp.arange(block_count, dtype=jnp.int32)[None, :]
    one_hot = jnp.logical_and(matches, live_slot[:, None]).astype(jnp.float32)

    def substep(x):
        mixed_adj = column_solve(x, inv, lower, factor)
        return advect(mixed_adj, east_part, north_part) * keep_factor

    total_steps = NCPL * NSUB
    peer_count = record_counts.shape[-1]
    plane = field_part.shape[1:]
    in_flight = {}
    saved = None
    for step in range(total_steps + SKEW):
        advanced = substep(field_part)
        if step < SKEW:
            field_part = jnp.where(is_ocean, field_part, advanced)
        else:
            field_part = advanced
        for c, (stage, value) in list(in_flight.items()):
            if stage == 0:
                value, _ = lax.optimization_barrier((value, field_part))
                in_flight[c] = (1, reduce_forcing(value, one_hot))
        air_done = step + 1
        if air_done <= total_steps and air_done % NSUB == 0:
            in_flight[air_done // NSUB - 1] = (
                0, couple(field_part, weight_table, source_block, peer_count))
        if step == total_steps - 1:
            saved = field_part
        ocean_done = step - SKEW + 1
        if ocean_done >= 1 and ocean_done % NSUB == 0:
            stage, parts = in_flight.pop(ocean_done // NSUB - 1)
            forcing = forcing_field(parts, plane)
            field_part = field_part.at[0].add(
                jnp.where(is_ocean, forcing * ocean_keep, jnp.zeros_like(forcing))
            )
    field_part = jnp.where(is_ocean, field_part, saved)
    return field_part[None]


def solution(mesh):
    in_specs = (
        P("sec", None, "lat", "lon"),
        P("sec", None, "lat", "lon"),
        P("sec", None, "lat", "lon"),
        P("sec", None, "lat", "lon"),
        P("lat", "lon"),
        P("sec", "lat", "lon", None, None, None),
        P("sec", "lat", "lon", None, None),
        P("sec", "lat", "lon", None, None),
        P("sec", "lat", "lon", None),
    )
    out_specs = P("sec", None, "lat", "lon")
    return jax.shard_map(local, mesh=mesh, in_specs=in_specs, out_specs=out_specs, check_vma=False)
```

```python
import jax
import jax.numpy as jnp
from jax import lax
from jax.experimental import pallas as pl
from jax.experimental.pallas import tpu as pltpu
from jax.sharding import PartitionSpec as P

NCPL = 4
NSUB = 2
SKEW = 2


def extended(block, sides, width, periodic):
    for axis, dim in sides:
        count = lax.axis_size(axis)
        forward = [(i, i + 1) for i in range(count - 1)]
        if periodic:
            forward.append((count - 1, 0))
        backward = [(target, source) for source, target in forward]
        low = lax.ppermute(
            lax.slice_in_dim(block, block.shape[dim] - width, None, axis=dim), axis, forward
        )
        high = lax.ppermute(lax.slice_in_dim(block, 0, width, axis=dim), axis, backward)
        block = jnp.concatenate([low, block, high], axis=dim)
    return block


def _factor_kernel(a_ref, inv_ref, b_ref, c_ref):
    lev = a_ref.shape[0]
    prior_c = jnp.zeros(a_ref.shape[1:], jnp.float32)
    zero = jnp.zeros(a_ref.shape[1:], jnp.float32)
    for k in range(lev):
        lower = a_ref[k] if k >= 1 else zero
        upper = a_ref[k + 1] if k + 1 < lev else zero
        centre = 1.0 + lower + upper
        pivot = centre + lower * prior_c
        inv = 1.0 / pivot
        factor = -upper / pivot
        inv_ref[k] = inv
        b_ref[k] = lower * inv
        c_ref[k] = factor
        prior_c = factor


def _solve_kernel(x_ref, inv_ref, b_ref, c_ref, o_ref):
    lev = x_ref.shape[0]

    def down(k, z):
        z = x_ref[k] * inv_ref[k] + b_ref[k] * z
        o_ref[k] = z
        return z

    def up(i, x):
        k = lev - 1 - i
        x = o_ref[k] - c_ref[k] * x
        o_ref[k] = x
        return x

    zero = jnp.zeros(x_ref.shape[1:], jnp.float32)
    lax.fori_loop(0, lev, down, zero, unroll=5)
    lax.fori_loop(0, lev, up, zero, unroll=5)


def factorise(coeff):
    shape = jax.ShapeDtypeStruct(coeff.shape, jnp.float32)
    size = coeff.size
    return pl.pallas_call(
        _factor_kernel,
        out_shape=(shape, shape, shape),
        cost_estimate=pl.CostEstimate(flops=8 * size, bytes_accessed=16 * size, transcendentals=0),
    )(coeff)


def column_solve(right, inv, lower, factor):
    size = right.size
    return pl.pallas_call(
        _solve_kernel,
        out_shape=jax.ShapeDtypeStruct(right.shape, jnp.float32),
        cost_estimate=pl.CostEstimate(flops=6 * size, bytes_accessed=20 * size, transcendentals=0),
    )(right, inv, lower, factor)


def advect(mixed_adj, east_speed, north_speed):
    east_flux = east_speed * mixed_adj
    north_flux = north_speed * mixed_adj
    east_rim = extended(east_flux, (("lon", 2),), 1, True)
    north_rim = extended(north_flux, (("lat", 1),), 1, False)
    east_diff = east_rim[:, :, 2:] - east_rim[:, :, :-2]
    north_diff = north_rim[:, 2:, :] - north_rim[:, :-2, :]
    return mixed_adj + 0.5 * (east_diff + north_diff)


def couple(field_part, weight_table, source_block, peer_count):
    block_cells = weight_table.shape[0]
    capacity = source_block.shape[-1]
    surface = field_part[-1].reshape(-1, block_cells)
    gathered = jnp.take(surface, source_block.reshape(-1), axis=0)
    contribution = jnp.einsum("diz,zi->dz", weight_table, gathered, precision=lax.Precision.HIGHEST)
    lat_count, lon_count = lax.axis_size("lat"), lax.axis_size("lon")
    section_count = lax.axis_size("sec")
    staged = contribution.reshape(block_cells, lat_count, lon_count, capacity)
    staged = lax.all_to_all(staged, "lon", split_axis=2, concat_axis=2, tiled=True)
    padded = jnp.zeros((block_cells, section_count) + staged.shape[1:], staged.dtype)
    padded = padded.at[:, section_count - 1].set(staged)
    padded = padded.reshape(block_cells, section_count * lat_count, lon_count, capacity)
    padded = lax.all_to_all(padded, ("sec", "lat"), split_axis=1, concat_axis=1, tiled=True)
    return padded[:, : (section_count - 1) * lat_count].reshape(block_cells, -1)


def reduce_forcing(received, one_hot):
    return jnp.dot(received, one_hot, precision=lax.Precision.HIGHEST, preferred_element_type=jnp.float32)


def forcing_field(total, shape):
    return total.T.reshape(shape)


def local(
    state, mixing, eastward, northward, sea_mask, weights, source_block, dest_block, record_counts
):
    section = lax.axis_index("sec")
    section_count = lax.axis_size("sec")
    is_ocean = section == section_count - 1
    ocean_keep = sea_mask.astype(jnp.float32)
    keep_factor = jnp.where(is_ocean, ocean_keep, jnp.ones_like(ocean_keep))
    field_part = state[0]
    inv, lower, factor = factorise(mixing[0].astype(jnp.float32))
    east_part = eastward[0].astype(jnp.float32)
    north_part = northward[0].astype(jnp.float32)

    weight_table = weights[0, 0, 0].astype(jnp.float32)
    block_count = field_part.shape[1] * field_part.shape[2] // weight_table.shape[0]
    capacity = source_block.shape[-1]
    live_slot = (
        jnp.arange(capacity, dtype=jnp.int32)[None, :] < record_counts[0, 0, 0][:, None]
    ).reshape(-1)
    matches = dest_block.reshape(-1)[:, None] == jnp.arange(block_count, dtype=jnp.int32)[None, :]
    own_hot = jnp.logical_and(matches, live_slot[:, None]).astype(jnp.float32)
    one_hot = jnp.concatenate(
        [lax.ppermute(own_hot, "sec", [(s, section_count - 1)]) for s in range(section_count - 1)],
        axis=0,
    )

    def substep(x):
        mixed_adj = column_solve(x, inv, lower, factor)
        return advect(mixed_adj, east_part, north_part) * keep_factor

    total_steps = NCPL * NSUB
    peer_count = record_counts.shape[-1]
    plane = field_part.shape[1:]
    in_flight = {}
    saved = None
    for step in range(total_steps + SKEW):
        advanced = substep(field_part)
        if step < SKEW:
            field_part = jnp.where(is_ocean, field_part, advanced)
        else:
            field_part = advanced
        for c, (stage, value) in list(in_flight.items()):
            if stage == 0:
                value, _ = lax.optimization_barrier((value, field_part))
                in_flight[c] = (1, reduce_forcing(value, one_hot))
        air_done = step + 1
        if air_done <= total_steps and air_done % NSUB == 0:
            in_flight[air_done // NSUB - 1] = (
                0, couple(field_part, weight_table, source_block, peer_count))
        if step == total_steps - 1:
            saved = field_part
        ocean_done = step - SKEW + 1
        if ocean_done >= 1 and ocean_done % NSUB == 0:
            stage, parts = in_flight.pop(ocean_done // NSUB - 1)
            forcing = forcing_field(parts, plane)
            field_part = field_part.at[0].add(
                jnp.where(is_ocean, forcing * ocean_keep, jnp.zeros_like(forcing))
            )
    field_part = jnp.where(is_ocean, field_part, saved)
    return field_part[None]


def solution(mesh):
    in_specs = (
        P("sec", None, "lat", "lon"),
        P("sec", None, "lat", "lon"),
        P("sec", None, "lat", "lon"),
        P("sec", None, "lat", "lon"),
        P("lat", "lon"),
        P("sec", "lat", "lon", None, None, None),
        P("sec", "lat", "lon", None, None),
        P("sec", "lat", "lon", None, None),
        P("sec", "lat", "lon", None),
    )
    out_specs = P("sec", None, "lat", "lon")
    return jax.shard_map(local, mesh=mesh, in_specs=in_specs, out_specs=out_specs, check_vma=False)
```

```python
import jax
import jax.numpy as jnp
from jax import lax
from jax.experimental import pallas as pl
from jax.experimental.pallas import tpu as pltpu
from jax.sharding import PartitionSpec as P

NCPL = 4
NSUB = 2
SKEW = 2


def extended(block, sides, width, periodic):
    for axis, dim in sides:
        count = lax.axis_size(axis)
        forward = [(i, i + 1) for i in range(count - 1)]
        if periodic:
            forward.append((count - 1, 0))
        backward = [(target, source) for source, target in forward]
        low = lax.ppermute(
            lax.slice_in_dim(block, block.shape[dim] - width, None, axis=dim), axis, forward
        )
        high = lax.ppermute(lax.slice_in_dim(block, 0, width, axis=dim), axis, backward)
        block = jnp.concatenate([low, block, high], axis=dim)
    return block


def _factor_kernel(a_ref, inv_ref, b_ref, c_ref):
    lev = a_ref.shape[0]
    prior_c = jnp.zeros(a_ref.shape[1:], jnp.float32)
    zero = jnp.zeros(a_ref.shape[1:], jnp.float32)
    for k in range(lev):
        lower = a_ref[k] if k >= 1 else zero
        upper = a_ref[k + 1] if k + 1 < lev else zero
        centre = 1.0 + lower + upper
        pivot = centre + lower * prior_c
        inv = 1.0 / pivot
        factor = -upper / pivot
        inv_ref[k] = inv
        b_ref[k] = lower * inv
        c_ref[k] = factor
        prior_c = factor


def _solve_kernel(x_ref, inv_ref, b_ref, c_ref, o_ref):
    lev = x_ref.shape[0]

    def down(k, z):
        z = x_ref[k] * inv_ref[k] + b_ref[k] * z
        o_ref[k] = z
        return z

    def up(i, x):
        k = lev - 1 - i
        x = o_ref[k] - c_ref[k] * x
        o_ref[k] = x
        return x

    zero = jnp.zeros(x_ref.shape[1:], jnp.float32)
    lax.fori_loop(0, lev, down, zero, unroll=5)
    lax.fori_loop(0, lev, up, zero, unroll=5)


def factorise(coeff):
    shape = jax.ShapeDtypeStruct(coeff.shape, jnp.float32)
    size = coeff.size
    return pl.pallas_call(
        _factor_kernel,
        out_shape=(shape, shape, shape),
        cost_estimate=pl.CostEstimate(flops=8 * size, bytes_accessed=16 * size, transcendentals=0),
    )(coeff)


def column_solve(right, inv, lower, factor):
    size = right.size
    return pl.pallas_call(
        _solve_kernel,
        out_shape=jax.ShapeDtypeStruct(right.shape, jnp.float32),
        cost_estimate=pl.CostEstimate(flops=6 * size, bytes_accessed=20 * size, transcendentals=0),
    )(right, inv, lower, factor)


def advect(mixed_adj, east_speed, north_speed):
    east_flux = east_speed * mixed_adj
    north_flux = north_speed * mixed_adj
    east_rim = extended(east_flux, (("lon", 2),), 1, True)
    north_rim = extended(north_flux, (("lat", 1),), 1, False)
    east_diff = east_rim[:, :, 2:] - east_rim[:, :, :-2]
    north_diff = north_rim[:, 2:, :] - north_rim[:, :-2, :]
    return mixed_adj + 0.5 * (east_diff + north_diff)


def couple(field_part, weight_table, source_block, peer_count):
    block_cells = weight_table.shape[0]
    capacity = source_block.shape[-1]
    surface = field_part[-1].reshape(-1, block_cells)
    gathered = jnp.take(surface, source_block.reshape(-1), axis=0)
    contribution = jnp.einsum("diz,zi->dz", weight_table, gathered, precision=lax.Precision.HIGHEST)
    lat_count, lon_count = lax.axis_size("lat"), lax.axis_size("lon")
    staged = contribution.reshape(block_cells, lat_count, lon_count, capacity)
    staged = lax.all_to_all(staged, "lon", split_axis=2, concat_axis=2, tiled=True)
    staged = lax.all_to_all(staged, "lat", split_axis=1, concat_axis=1, tiled=True)
    return staged.reshape(block_cells, peer_count, capacity)


def reduce_forcing(received, one_hot):
    block_cells = received.shape[0]
    arrived = received.reshape(block_cells, -1)
    accumulated = jnp.dot(
        arrived, one_hot, precision=lax.Precision.HIGHEST, preferred_element_type=jnp.float32
    )
    section_count = lax.axis_size("sec")
    if section_count != 4:
        return [lax.ppermute(accumulated, "sec", [(s, section_count - 1)]) for s in range(section_count - 1)]
    first = lax.ppermute(accumulated, "sec", [(0, 3), (1, 2)])
    second = lax.ppermute(accumulated + first, "sec", [(2, 3)])
    return [first, second]


def forcing_field(parts, shape):
    total = parts[0]
    for part in parts[1:]:
        total = total + part
    return total.T.reshape(shape)


def local(
    state, mixing, eastward, northward, sea_mask, weights, source_block, dest_block, record_counts
):
    section = lax.axis_index("sec")
    section_count = lax.axis_size("sec")
    is_ocean = section == section_count - 1
    ocean_keep = sea_mask.astype(jnp.float32)
    keep_factor = jnp.where(is_ocean, ocean_keep, jnp.ones_like(ocean_keep))
    field_part = state[0]
    inv, lower, factor = factorise(mixing[0].astype(jnp.float32))
    east_part = eastward[0].astype(jnp.float32)
    north_part = northward[0].astype(jnp.float32)

    weight_table = weights[0, 0, 0].astype(jnp.float32)
    block_count = field_part.shape[1] * field_part.shape[2] // weight_table.shape[0]
    capacity = source_block.shape[-1]
    live_slot = (
        jnp.arange(capacity, dtype=jnp.int32)[None, :] < record_counts[0, 0, 0][:, None]
    ).reshape(-1)
    matches = dest_block.reshape(-1)[:, None] == jnp.arange(block_count, dtype=jnp.int32)[None, :]
    one_hot = jnp.logical_and(matches, live_slot[:, None]).astype(jnp.float32)

    def substep(x):
        mixed_adj = column_solve(x, inv, lower, factor)
        return advect(mixed_adj, east_part, north_part) * keep_factor

    total_steps = NCPL * NSUB
    peer_count = record_counts.shape[-1]
    plane = field_part.shape[1:]
    in_flight = {}
    saved = None
    for step in range(total_steps + SKEW):
        advanced = substep(field_part)
        if step < SKEW:
            field_part = jnp.where(is_ocean, field_part, advanced)
        else:
            field_part = advanced
        for c, (stage, value) in list(in_flight.items()):
            if stage == 0:
                value, _ = lax.optimization_barrier((value, field_part))
                in_flight[c] = (1, reduce_forcing(value, one_hot))
        air_done = step + 1
        if air_done <= total_steps and air_done % NSUB == 0:
            in_flight[air_done // NSUB - 1] = (
                0, couple(field_part, weight_table, source_block, peer_count))
        if step == total_steps - 1:
            saved = field_part
        ocean_done = step - SKEW + 1
        if ocean_done >= 1 and ocean_done % NSUB == 0:
            stage, parts = in_flight.pop(ocean_done // NSUB - 1)
            forcing = forcing_field(parts, plane)
            field_part = field_part.at[0].add(
                jnp.where(is_ocean, forcing * ocean_keep, jnp.zeros_like(forcing))
            )
    field_part = jnp.where(is_ocean, field_part, saved)
    return field_part[None]


def solution(mesh):
    in_specs = (
        P("sec", None, "lat", "lon"),
        P("sec", None, "lat", "lon"),
        P("sec", None, "lat", "lon"),
        P("sec", None, "lat", "lon"),
        P("lat", "lon"),
        P("sec", "lat", "lon", None, None, None),
        P("sec", "lat", "lon", None, None),
        P("sec", "lat", "lon", None, None),
        P("sec", "lat", "lon", None),
    )
    out_specs = P("sec", None, "lat", "lon")
    return jax.shard_map(local, mesh=mesh, in_specs=in_specs, out_specs=out_specs, check_vma=False)
```
